256 devices in a mesh: adapter: 32 (over z, y), tensor: 8 (over x, core).
Axes of the slice: x: 4, y: 4, z: 8, core: 2. Of those that a mesh axis runs over, the one named last changes fastest.
Arguments:
- hidden: bfloat16 [3072, 2, 8192], P('adapter'), may hold values from -6 to 6
- input_norm_gain: bfloat16 [8192], replicated, may hold values from 0.25 to 1.75
- key_value_weight: bfloat16 [8192, 2, 1024], P(None, None, 'tensor'), may hold values from -0.0625 to 0.0625
- adapter_down_weight: bfloat16 [128, 8192, 128], P('adapter', 'tensor'), may hold values from -0.0625 to 0.0625
- adapter_up_weight: bfloat16 [128, 2, 64, 1024], P('adapter', None, None, 'tensor'), may hold values from -0.375 to 0.375
- request_adapter: int32 [3072], P('adapter'), may hold values from 0 to 127, as said below
- queries: bfloat16 [3072, 2, 8192], P('adapter', None, 'tensor'), may hold values from -100 to 100
- cached_key_rows: bfloat16 [3072, 64, 1024], P('adapter', None, 'tensor'), may hold values from -5 to 5
- cached_value_rows: bfloat16 [3072, 64, 1024], P('adapter', None, 'tensor'), may hold values from -6 to 6
- cached_length: int32 [3072], P('adapter'), may hold values from 2 to 64, as said below
Outputs:
- new_keys: bfloat16 [3072, 2, 1024], P('adapter', None, 'tensor')
- new_values: bfloat16 [3072, 2, 1024], P('adapter', None, 'tensor')
- attended: bfloat16 [3072, 2, 8192], P('adapter', None, 'tensor')
The draws below stay inside these ranges and needn't reach their ends.
Inputs may be any that keep to these rules, and one draw needn't show every extreme that they name: `request_adapter`: adapter a is held by adapter index a // 4. Of the requests on one adapter index at most 6 name adapters held by one adapter index, and in every draw one adapter index is named by exactly 6 requests of every adapter index. `cached_length`: some request has exactly 64 cached tokens.
All inputs are finite; a program needn't handle non-finite values.
Results may differ from the reference program's by a relative error of at most 0.0055.
Values may be sent and summed in bfloat16 or wider, within the bound.
No kernel may reach another device: no remote copies, remote signals or barrier semaphores. Data moves between devices by JAX's collectives and lax.ppermute only.
A program may use at most 128 MiB of HBM per device.

```python
import jax
import jax.numpy as jnp
from jax import lax

MODEL_DIM = 8192
KEY_VALUE_HEADS = 8
HEAD_DIM = 128
GQ = 8
ADAPTER_RANK = 64
NEW_TOKENS = 2
REQUESTS_PER_SLOT = 96
CTX = 64
AD_DEV = 4
REQUESTS = 3072
ADAPTER_TOTAL = 128


def shared_keys(key):
    base_keys = jax.random.normal(jax.random.fold_in(key, 23), (REQUESTS, CTX, KEY_VALUE_HEADS * HEAD_DIM), jnp.float32)
    base_keys = jnp.clip(base_keys, -5.0, 5.0)
    return base_keys


def draw_cached_key_rows(key, part):
    return shared_keys(key).astype(jnp.bfloat16)


def draw_queries(key, part):
    fresh_draw = jax.random.normal(jax.random.fold_in(key, 24), (REQUESTS, NEW_TOKENS, KEY_VALUE_HEADS * GQ * HEAD_DIM), jnp.float32)
    fresh_draw = jnp.clip(fresh_draw, -5.0, 5.0)
    return fresh_draw.astype(jnp.bfloat16)


def draw_cached_length(key, part):
    lengths = jax.random.randint(jax.random.fold_in(key, 31), (REQUESTS,), 2, CTX + 1)
    longest = jax.random.randint(jax.random.fold_in(key, 32), (), 0, REQUESTS)
    return jnp.where(jnp.arange(REQUESTS, dtype=jnp.int32) == longest, CTX, lengths).astype(jnp.int32)


def draw_request_adapter(key, part):
    block_list = REQUESTS // REQUESTS_PER_SLOT
    capacity = 2 * REQUESTS_PER_SLOT // block_list
    slot_total = block_list * capacity
    slot_ids = jnp.arange(slot_total, dtype=jnp.int32)
    slot_owner = slot_ids // capacity
    first_slot = 0
    last_slot = (block_list - 1) * capacity
    hot_owner = jax.random.randint(jax.random.fold_in(key, 41), (block_list,), 0, 4) == 0
    full_owner = jax.random.randint(jax.random.fold_in(key, 42), (), 0, block_list)
    scores = jax.random.randint(jax.random.fold_in(key, 43), (block_list, slot_total), 0, 1 << 20)
    scores = scores + jnp.where(hot_owner[slot_owner], 1 << 20, 0)[None, :]
    scores = scores + jnp.where(slot_owner == full_owner, 1 << 22, 0)[None, :]
    forced_slot = (slot_ids == first_slot) | (slot_ids == last_slot)
    block_zero = jnp.arange(block_list, dtype=jnp.int32) == 0
    scores = scores + jnp.where(block_zero[:, None] & forced_slot[None, :], 1 << 23, 0)
    ranked = jnp.argsort(-scores, axis=1, stable=True)[:, :REQUESTS_PER_SLOT]
    shuffle = jnp.argsort(jax.random.randint(jax.random.fold_in(key, 44), (block_list, REQUESTS_PER_SLOT), 0, 1 << 30), axis=1, stable=True)
    chosen = jnp.take_along_axis(ranked, shuffle, axis=1)
    owners = slot_owner[chosen]
    first_pick = jax.random.randint(jax.random.fold_in(key, 45), (block_list, REQUESTS_PER_SLOT), 0, AD_DEV)
    second_pick = jax.random.randint(jax.random.fold_in(key, 46), (block_list, REQUESTS_PER_SLOT), 0, AD_DEV)
    offsets = jax.random.randint(jax.random.fold_in(key, 47), (block_list,), 0, AD_DEV)
    local_pick = (jnp.minimum(first_pick, second_pick) + offsets[owners]) % AD_DEV
    local_pick = jnp.where(block_zero[:, None] & (chosen == first_slot), 0, local_pick)
    local_pick = jnp.where(block_zero[:, None] & (chosen == last_slot), AD_DEV - 1, local_pick)
    return (owners * AD_DEV + local_pick).reshape(REQUESTS).astype(jnp.int32)


def block_levels(stream_key, dims, shards, least, high):
    def one(dim, shards_of):
        heights = jax.random.uniform(jax.random.fold_in(jax.random.fold_in(stream_key, 6), dim), (shards_of,), jnp.float32, least / len(shards), high / len(shards))
        return jnp.repeat(jnp.exp(heights), dims[dim] // shards_of).reshape((-1,) + (1,) * (len(dims) - dim - 1))

    loudness = one(*shards[0])
    for cut in shards[1:]:
        loudness = loudness * one(*cut)
    return loudness


def noise(rng, shape, deviation, most, shards=(), held_as=jnp.bfloat16):
    entries = jax.random.normal(rng, shape, jnp.float32) * deviation
    if len(shards) > 0:
        entries = block_levels(rng, shape, shards, -0.22, 0.18) * entries
    return jnp.clip(entries, min=-most, max=most).astype(held_as)


def setup_inputs(seed: int = 0) -> dict:
    key_of = jax.random.split(jax.random.key(seed), 11)
    return {
        "hidden": noise(key_of[0], (REQUESTS, NEW_TOKENS, MODEL_DIM), 1.0, 6.0, ((0, 32),)),
        "input_norm_gain": jnp.clip(1.0 + 0.15 * jax.random.normal(key_of[1], (MODEL_DIM,), jnp.float32), 0.25, 1.75).astype(jnp.bfloat16),
        "key_value_weight": noise(key_of[2], (MODEL_DIM, 2, KEY_VALUE_HEADS * HEAD_DIM), MODEL_DIM ** -0.5, 0.0625, ((2, 8),)),
        "adapter_down_weight": noise(key_of[3], (ADAPTER_TOTAL, MODEL_DIM, 2 * ADAPTER_RANK), MODEL_DIM ** -0.5, 0.0625, ((0, 32), (1, 8))),
        "adapter_up_weight": noise(key_of[4], (ADAPTER_TOTAL, 2, ADAPTER_RANK, KEY_VALUE_HEADS * HEAD_DIM), (4 * ADAPTER_RANK) ** -0.5, 0.375, ((0, 32), (3, 8))),
        "request_adapter": draw_request_adapter(jax.random.fold_in(key_of[10], 71), 0),
        "queries": draw_queries(jax.random.fold_in(key_of[10], 71), 0),
        "cached_key_rows": draw_cached_key_rows(jax.random.fold_in(key_of[10], 71), 0),
        "cached_value_rows": noise(key_of[8], (REQUESTS, CTX, KEY_VALUE_HEADS * HEAD_DIM), 1.0, 6.0, ((0, 32), (2, 8))),
        "cached_length": draw_cached_length(jax.random.fold_in(key_of[10], 71), 0),
    }


epsilon = 1e-05
rope_base = 500000.0

def rotate_keys(key_vecs, positions):
    head_size = key_vecs.shape[-1]
    half_size = head_size // 2
    inverse = rope_base ** (-(jnp.arange(half_size, dtype=jnp.float32) * 2.0 / head_size))
    angles = positions[..., None] * inverse
    cosine = jnp.cos(angles)
    sine_part = jnp.sin(angles)
    first_half = key_vecs[..., :half_size]
    second = key_vecs[..., half_size:]
    return jnp.concatenate([first_half * cosine - second * sine_part, second * cosine + first_half * sine_part], axis=-1)

def normalize(hidden, input_norm_gain):
    values = hidden.astype(jnp.float32)
    meansq = lax.optimization_barrier(jnp.mean(values * values, axis=-1, keepdims=True))
    return (values * lax.rsqrt(meansq + epsilon) * input_norm_gain.astype(jnp.float32)).astype(jnp.bfloat16)

def attend(queries, cached_key_rows, cached_value_rows, cached_length, new_keys, new_values):
    score_scale = float(HEAD_DIM) ** (-0.5)
    query_vecs = queries.reshape(REQUESTS, NEW_TOKENS, KEY_VALUE_HEADS, GQ, HEAD_DIM).astype(jnp.float32)
    cache_vecs = cached_key_rows.reshape(REQUESTS, CTX, KEY_VALUE_HEADS, HEAD_DIM).astype(jnp.float32)
    fresh_vecs = new_keys.reshape(REQUESTS, NEW_TOKENS, KEY_VALUE_HEADS, HEAD_DIM).astype(jnp.float32)
    cache_scores = jnp.einsum('rthgd,rjhd->rthgj', query_vecs, cache_vecs) * score_scale
    slot_live = jnp.arange(CTX, dtype=jnp.int32)[None, :] < cached_length[:, None]
    cache_scores = jnp.where(slot_live[:, None, None, None, :], cache_scores, -1e+30)
    fresh_scores = jnp.einsum('rthgd,rshd->rthgs', query_vecs, fresh_vecs) * score_scale
    causal = jnp.arange(NEW_TOKENS, dtype=jnp.int32)[:, None] >= jnp.arange(NEW_TOKENS, dtype=jnp.int32)[None, :]
    fresh_scores = jnp.where(causal[None, :, None, None, :], fresh_scores, -1e+30)
    top_score = jnp.maximum(lax.optimization_barrier(jnp.max(cache_scores, axis=-1)), lax.optimization_barrier(jnp.max(fresh_scores, axis=-1)))[..., None]
    cache_weights = jnp.exp(cache_scores - top_score)
    fresh_weights = jnp.exp(fresh_scores - top_score)
    total_weight = lax.optimization_barrier(jnp.sum(cache_weights, axis=-1, keepdims=True)) + lax.optimization_barrier(jnp.sum(fresh_weights, axis=-1, keepdims=True))
    cache_probs = (cache_weights / total_weight).astype(jnp.bfloat16)
    fresh_probs = (fresh_weights / total_weight).astype(jnp.bfloat16)
    cache_vals = cached_value_rows.reshape(REQUESTS, CTX, KEY_VALUE_HEADS, HEAD_DIM).astype(jnp.float32)
    fresh_vals = new_values.reshape(REQUESTS, NEW_TOKENS, KEY_VALUE_HEADS, HEAD_DIM).astype(jnp.float32)
    mixed_out = jnp.einsum('rthgj,rjhd->rthgd', cache_probs.astype(jnp.float32), cache_vals)
    mixed_out = mixed_out + jnp.einsum('rthgs,rshd->rthgd', fresh_probs.astype(jnp.float32), fresh_vals)
    return mixed_out.reshape(REQUESTS, NEW_TOKENS, KEY_VALUE_HEADS * GQ * HEAD_DIM).astype(jnp.bfloat16)

def reference(hidden, input_norm_gain, key_value_weight, adapter_down_weight, adapter_up_weight, request_adapter, queries, cached_key_rows, cached_value_rows, cached_length):
    normed_input = normalize(hidden, input_norm_gain)
    flat_rows = normed_input.reshape(REQUESTS * NEW_TOKENS, MODEL_DIM)
    base_proj = jnp.dot(flat_rows, key_value_weight.reshape(MODEL_DIM, 2 * KEY_VALUE_HEADS * HEAD_DIM), preferred_element_type=jnp.float32)
    base_proj = base_proj.reshape(REQUESTS, NEW_TOKENS, 2, KEY_VALUE_HEADS * HEAD_DIM)
    block_list = REQUESTS // REQUESTS_PER_SLOT

    def adapter_block(operand_list):
        block_rows, block_numbers = operand_list
        down_matrices = adapter_down_weight[block_numbers].astype(jnp.float32)
        rank_hidden = jnp.einsum('rtd,rdk->rtk', block_rows.astype(jnp.float32), down_matrices).astype(jnp.bfloat16)
        up_matrices = adapter_up_weight[block_numbers].astype(jnp.float32)
        key_part = jnp.einsum('rtk,rkh->rth', rank_hidden[..., :ADAPTER_RANK].astype(jnp.float32), up_matrices[:, 0])
        value_part = jnp.einsum('rtk,rkh->rth', rank_hidden[..., ADAPTER_RANK:].astype(jnp.float32), up_matrices[:, 1])
        return jnp.stack([key_part, value_part], axis=2)
    adapter_update = lax.map(adapter_block, (normed_input.reshape(block_list, REQUESTS_PER_SLOT, NEW_TOKENS, MODEL_DIM), request_adapter.reshape(block_list, REQUESTS_PER_SLOT)))
    projected_output = base_proj + adapter_update.reshape(REQUESTS, NEW_TOKENS, 2, KEY_VALUE_HEADS * HEAD_DIM)
    positions = (cached_length[:, None] + jnp.arange(NEW_TOKENS, dtype=jnp.int32)[None, :]).astype(jnp.float32)
    key_vecs = rotate_keys(projected_output[:, :, 0].reshape(REQUESTS, NEW_TOKENS, KEY_VALUE_HEADS, HEAD_DIM), positions[:, :, None])
    new_keys = key_vecs.reshape(REQUESTS, NEW_TOKENS, KEY_VALUE_HEADS * HEAD_DIM).astype(jnp.bfloat16)
    new_values = projected_output[:, :, 1].astype(jnp.bfloat16)
    attended = attend(queries, cached_key_rows, cached_value_rows, cached_length, new_keys, new_values)
    return (new_keys, new_values, attended)
```

```python
import jax
import jax.numpy as jnp
from jax import lax
from jax.sharding import PartitionSpec as P

HEAD_DIM = 128
SLOT_CAPACITY = 6


epsilon = 1e-05
rope_base = 500000.0


def rotate_keys(key_vecs, positions):
    head_size = key_vecs.shape[-1]
    half_size = head_size // 2
    inverse = rope_base ** (-(jnp.arange(half_size, dtype=jnp.float32) * 2.0 / head_size))
    angles = positions[..., None] * inverse
    cosine = jnp.cos(angles)
    sine_part = jnp.sin(angles)
    first_half = key_vecs[..., :half_size]
    second = key_vecs[..., half_size:]
    return jnp.concatenate(
        [first_half * cosine - second * sine_part, second * cosine + first_half * sine_part],
        axis=-1,
    )


def normalize(hidden, input_norm_gain):
    values = hidden.astype(jnp.float32)
    meansq = jnp.mean(values * values, axis=-1, keepdims=True)
    return (values * lax.rsqrt(meansq + epsilon) * input_norm_gain.astype(jnp.float32)).astype(
        jnp.bfloat16
    )


def attend(
    queries, cached_key_rows, cached_value_rows, cached_length, new_keys, new_values, head_size
):
    row_total, token_total, query_width = queries.shape
    context = cached_key_rows.shape[1]
    kv_local = cached_key_rows.shape[2] // head_size
    group_size = query_width // (kv_local * head_size)
    score_scale = float(head_size) ** (-0.5)
    query_vecs = queries.reshape(row_total, token_total, kv_local, group_size, head_size)
    cache_vecs = cached_key_rows.reshape(row_total, context, kv_local, head_size)
    fresh_vecs = new_keys.reshape(row_total, token_total, kv_local, head_size)
    cache_scores = (
        jnp.einsum("rthgd,rjhd->rthgj", query_vecs, cache_vecs, preferred_element_type=jnp.float32)
        * score_scale
    )
    slot_live = jnp.arange(context, dtype=jnp.int32)[None, :] < cached_length[:, None]
    cache_scores = jnp.where(slot_live[:, None, None, None, :], cache_scores, -1e30)
    fresh_scores = (
        jnp.einsum("rthgd,rshd->rthgs", query_vecs, fresh_vecs, preferred_element_type=jnp.float32)
        * score_scale
    )
    causal = (
        jnp.arange(token_total, dtype=jnp.int32)[:, None]
        >= jnp.arange(token_total, dtype=jnp.int32)[None, :]
    )
    fresh_scores = jnp.where(causal[None, :, None, None, :], fresh_scores, -1e30)
    top_score = jnp.maximum(jnp.max(cache_scores, axis=-1), jnp.max(fresh_scores, axis=-1))[
        ..., None
    ]
    cache_weights = jnp.exp(cache_scores - top_score)
    fresh_weights = jnp.exp(fresh_scores - top_score)
    total_weight = jnp.sum(cache_weights, axis=-1, keepdims=True) + jnp.sum(
        fresh_weights, axis=-1, keepdims=True
    )
    cache_probs = (cache_weights / total_weight).astype(jnp.bfloat16)
    fresh_probs = (fresh_weights / total_weight).astype(jnp.bfloat16)
    cache_vals = cached_value_rows.reshape(row_total, context, kv_local, head_size)
    fresh_vals = new_values.reshape(row_total, token_total, kv_local, head_size)
    mixed_out = jnp.einsum(
        "rthgj,rjhd->rthgd", cache_probs, cache_vals, preferred_element_type=jnp.float32
    )
    mixed_out = mixed_out + jnp.einsum(
        "rthgs,rshd->rthgd", fresh_probs, fresh_vals, preferred_element_type=jnp.float32
    )
    return mixed_out.reshape(row_total, token_total, query_width).astype(jnp.bfloat16)


def body(
    hidden,
    input_norm_gain,
    key_value_weight,
    adapter_down_weight,
    adapter_up_weight,
    request_adapter,
    queries,
    cached_key_rows,
    cached_value_rows,
    cached_length,
):
    row_count, token_count, model_width = hidden.shape
    feature_total = adapter_down_weight.shape[1]
    adapter_number = adapter_down_weight.shape[0]
    rank_total = adapter_down_weight.shape[2]
    rank_width = adapter_up_weight.shape[2]
    column_count = key_value_weight.shape[2]
    owner_count = lax.axis_size("adapter")
    cap = SLOT_CAPACITY
    slot_total = owner_count * cap

    normed_input = normalize(hidden, input_norm_gain)
    base_proj = jnp.dot(
        normed_input.reshape(row_count * token_count, model_width),
        key_value_weight.reshape(model_width, 2 * column_count),
        preferred_element_type=jnp.float32,
    )
    base_proj = base_proj.reshape(row_count, token_count, 2, column_count)

    owner_of = request_adapter // adapter_number
    local_adapter = request_adapter - owner_of * adapter_number
    row_ids = jnp.arange(row_count, dtype=jnp.int32)
    same_owner = owner_of[:, None] == owner_of[None, :]
    earlier = row_ids[None, :] < row_ids[:, None]
    rank_in_owner = jnp.sum((same_owner & earlier).astype(jnp.int32), axis=1)
    slot_of = owner_of * cap + rank_in_owner
    pick = (slot_of[None, :] == jnp.arange(slot_total, dtype=jnp.int32)[:, None]).astype(
        jnp.bfloat16
    )

    feature_start = lax.axis_index("tensor") * feature_total
    own_features = lax.dynamic_slice_in_dim(normed_input, feature_start, feature_total, 2)
    packed = jnp.dot(
        pick,
        own_features.reshape(row_count, token_count * feature_total),
        preferred_element_type=jnp.float32,
    ).astype(jnp.bfloat16)
    packed = packed.reshape(owner_count, cap * token_count, feature_total)
    slot_adapter = jnp.dot(
        pick, local_adapter.astype(jnp.bfloat16), preferred_element_type=jnp.float32
    ).astype(jnp.bfloat16)
    id_row = jnp.zeros((owner_count, 1, feature_total), jnp.bfloat16)
    id_row = lax.dynamic_update_slice(
        id_row, slot_adapter.reshape(owner_count, 1, cap), (0, 0, 0)
    )
    send = jnp.concatenate([packed, id_row], axis=1)
    recv = lax.all_to_all(send, "adapter", 0, 0, tiled=True)

    got_rows = recv[:, : cap * token_count].reshape(slot_total, token_count, feature_total)
    got_adapter = recv[:, cap * token_count, :cap].reshape(slot_total).astype(jnp.int32)
    selector = (
        got_adapter[:, None] == jnp.arange(adapter_number, dtype=jnp.int32)[None, :]
    ).astype(jnp.float32)

    down_all = jnp.einsum(
        "euz,nzs->euns", got_rows, adapter_down_weight, preferred_element_type=jnp.float32
    )
    partial_rank = jnp.sum(down_all * selector[:, None, :, None], axis=2)
    rank_hidden = lax.psum(partial_rank, "tensor").astype(jnp.bfloat16)

    rank_selector = selector.astype(jnp.bfloat16)
    masked = rank_hidden[:, :, None, :] * rank_selector[:, None, :, None]
    key_part = jnp.einsum(
        "gled,edb->glb",
        masked[..., :rank_width],
        adapter_up_weight[:, 0],
        preferred_element_type=jnp.float32,
    )
    value_part = jnp.einsum(
        "gled,edb->glb",
        masked[..., rank_width:],
        adapter_up_weight[:, 1],
        preferred_element_type=jnp.float32,
    )
    delta_slots = jnp.stack([key_part, value_part], axis=2)
    delta_send = delta_slots.reshape(owner_count, cap * token_count * 2, column_count)
    delta_recv = lax.all_to_all(delta_send, "adapter", 0, 0, tiled=True)
    delta_rows = delta_recv.reshape(slot_total, token_count * 2 * column_count)
    adapter_update = jnp.take(delta_rows, slot_of, axis=0).reshape(
        row_count, token_count, 2, column_count
    )

    projected_output = base_proj + adapter_update
    positions = (cached_length[:, None] + jnp.arange(token_count, dtype=jnp.int32)[None, :]).astype(
        jnp.float32
    )
    kv_local = column_count // HEAD_DIM
    key_vecs = rotate_keys(
        projected_output[:, :, 0].reshape(row_count, token_count, kv_local, HEAD_DIM),
        positions[:, :, None],
    )
    new_keys = key_vecs.reshape(row_count, token_count, column_count).astype(jnp.bfloat16)
    new_values = projected_output[:, :, 1].astype(jnp.bfloat16)
    attended = attend(
        queries, cached_key_rows, cached_value_rows, cached_length, new_keys, new_values, HEAD_DIM
    )
    return (new_keys, new_values, attended)


def solution(mesh):
    in_specs = (
        P("adapter", None, None),
        P(),
        P(None, None, "tensor"),
        P("adapter", "tensor", None),
        P("adapter", None, None, "tensor"),
        P("adapter"),
        P("adapter", None, "tensor"),
        P("adapter", None, "tensor"),
        P("adapter", None, "tensor"),
        P("adapter"),
    )
    out_specs = (
        P("adapter", None, "tensor"),
        P("adapter", None, "tensor"),
        P("adapter", None, "tensor"),
    )
    return jax.shard_map(body, mesh=mesh, in_specs=in_specs, out_specs=out_specs, check_vma=False)
```

```python
import jax
import jax.numpy as jnp
from jax import lax
from jax.sharding import PartitionSpec as P

HEAD_DIM = 128
SLOT_CAPACITY = 6


epsilon = 1e-05
rope_base = 500000.0


def rotate_keys(key_vecs, positions):
    head_size = key_vecs.shape[-1]
    half_size = head_size // 2
    inverse = rope_base ** (-(jnp.arange(half_size, dtype=jnp.float32) * 2.0 / head_size))
    angles = positions[..., None] * inverse
    cosine = jnp.cos(angles)
    sine_part = jnp.sin(angles)
    first_half = key_vecs[..., :half_size]
    second = key_vecs[..., half_size:]
    return jnp.concatenate(
        [first_half * cosine - second * sine_part, second * cosine + first_half * sine_part],
        axis=-1,
    )


def normalize(hidden, input_norm_gain):
    values = hidden.astype(jnp.float32)
    meansq = jnp.mean(values * values, axis=-1, keepdims=True)
    return (values * lax.rsqrt(meansq + epsilon) * input_norm_gain.astype(jnp.float32)).astype(
        jnp.bfloat16
    )


def attend(
    queries, cached_key_rows, cached_value_rows, cached_length, new_keys, new_values, head_size
):
    row_total, token_total, query_width = queries.shape
    context = cached_key_rows.shape[1]
    kv_local = cached_key_rows.shape[2] // head_size
    group_size = query_width // (kv_local * head_size)
    score_scale = float(head_size) ** (-0.5)
    query_vecs = queries.reshape(row_total, token_total, kv_local, group_size, head_size)
    cache_vecs = cached_key_rows.reshape(row_total, context, kv_local, head_size)
    fresh_vecs = new_keys.reshape(row_total, token_total, kv_local, head_size)
    cache_scores = (
        jnp.einsum("rthgd,rjhd->rthgj", query_vecs, cache_vecs, preferred_element_type=jnp.float32)
        * score_scale
    )
    slot_live = jnp.arange(context, dtype=jnp.int32)[None, :] < cached_length[:, None]
    cache_scores = jnp.where(slot_live[:, None, None, None, :], cache_scores, -1e30)
    fresh_scores = (
        jnp.einsum("rthgd,rshd->rthgs", query_vecs, fresh_vecs, preferred_element_type=jnp.float32)
        * score_scale
    )
    causal = (
        jnp.arange(token_total, dtype=jnp.int32)[:, None]
        >= jnp.arange(token_total, dtype=jnp.int32)[None, :]
    )
    fresh_scores = jnp.where(causal[None, :, None, None, :], fresh_scores, -1e30)
    top_score = jnp.maximum(jnp.max(cache_scores, axis=-1), jnp.max(fresh_scores, axis=-1))[
        ..., None
    ]
    cache_weights = jnp.exp(cache_scores - top_score)
    fresh_weights = jnp.exp(fresh_scores - top_score)
    total_weight = jnp.sum(cache_weights, axis=-1, keepdims=True) + jnp.sum(
        fresh_weights, axis=-1, keepdims=True
    )
    cache_probs = (cache_weights / total_weight).astype(jnp.bfloat16)
    fresh_probs = (fresh_weights / total_weight).astype(jnp.bfloat16)
    cache_vals = cached_value_rows.reshape(row_total, context, kv_local, head_size)
    fresh_vals = new_values.reshape(row_total, token_total, kv_local, head_size)
    mixed_out = jnp.einsum(
        "rthgj,rjhd->rthgd", cache_probs, cache_vals, preferred_element_type=jnp.float32
    )
    mixed_out = mixed_out + jnp.einsum(
        "rthgs,rshd->rthgd", fresh_probs, fresh_vals, preferred_element_type=jnp.float32
    )
    return mixed_out.reshape(row_total, token_total, query_width).astype(jnp.bfloat16)


def body(
    hidden,
    input_norm_gain,
    key_value_weight,
    adapter_down_weight,
    adapter_up_weight,
    request_adapter,
    queries,
    cached_key_rows,
    cached_value_rows,
    cached_length,
):
    row_count, token_count, model_width = hidden.shape
    feature_total = adapter_down_weight.shape[1]
    adapter_number = adapter_down_weight.shape[0]
    rank_total = adapter_down_weight.shape[2]
    rank_width = adapter_up_weight.shape[2]
    column_count = key_value_weight.shape[2]
    owner_count = lax.axis_size("adapter")
    cap = SLOT_CAPACITY
    slot_total = owner_count * cap

    values = hidden.astype(jnp.float32)
    meansq = jnp.mean(values * values, axis=-1, keepdims=True)
    row_scale = lax.rsqrt(meansq + epsilon)
    normed_input = (values * row_scale * input_norm_gain.astype(jnp.float32)).astype(jnp.bfloat16)
    base_proj = jnp.dot(
        normed_input.reshape(row_count * token_count, model_width),
        key_value_weight.reshape(model_width, 2 * column_count),
        preferred_element_type=jnp.float32,
    )
    base_proj = lax.optimization_barrier(base_proj.reshape(row_count, token_count, 2, column_count))

    owner_of = request_adapter // adapter_number
    local_adapter = request_adapter - owner_of * adapter_number
    row_ids = jnp.arange(row_count, dtype=jnp.int32)
    same_owner = owner_of[:, None] == owner_of[None, :]
    earlier = row_ids[None, :] < row_ids[:, None]
    rank_in_owner = jnp.sum((same_owner & earlier).astype(jnp.int32), axis=1)
    slot_of = owner_of * cap + rank_in_owner
    pick = (slot_of[None, :] == jnp.arange(slot_total, dtype=jnp.int32)[:, None]).astype(
        jnp.bfloat16
    )

    feature_start = lax.axis_index("tensor") * feature_total
    hidden_shard = lax.dynamic_slice_in_dim(hidden, feature_start, feature_total, 2)
    gain_shard = lax.dynamic_slice_in_dim(input_norm_gain, feature_start, feature_total, 0)
    own_features = (
        hidden_shard.astype(jnp.float32) * row_scale * gain_shard.astype(jnp.float32)
    ).astype(jnp.bfloat16)
    packed = jnp.dot(
        pick,
        own_features.reshape(row_count, token_count * feature_total),
        preferred_element_type=jnp.float32,
    ).astype(jnp.bfloat16)
    packed = packed.reshape(owner_count, cap * token_count, feature_total)
    slot_adapter = jnp.dot(
        pick, local_adapter.astype(jnp.bfloat16), preferred_element_type=jnp.float32
    ).astype(jnp.bfloat16)
    id_row = jnp.zeros((owner_count, 1, feature_total), jnp.bfloat16)
    id_row = lax.dynamic_update_slice(
        id_row, slot_adapter.reshape(owner_count, 1, cap), (0, 0, 0)
    )
    send = jnp.concatenate([packed, id_row], axis=1)
    recv = lax.all_to_all(send, "adapter", 0, 0, tiled=True)

    got_rows = recv[:, : cap * token_count].reshape(slot_total, token_count, feature_total)
    got_adapter = recv[:, cap * token_count, :cap].reshape(slot_total).astype(jnp.int32)
    selector = (
        got_adapter[:, None] == jnp.arange(adapter_number, dtype=jnp.int32)[None, :]
    ).astype(jnp.float32)

    down_all = jnp.einsum(
        "euz,nzs->euns", got_rows, adapter_down_weight, preferred_element_type=jnp.float32
    )
    partial_rank = jnp.sum(down_all * selector[:, None, :, None], axis=2)
    rank_hidden = lax.psum(partial_rank, "tensor").astype(jnp.bfloat16)

    rank_selector = selector.astype(jnp.bfloat16)
    masked = rank_hidden[:, :, None, :] * rank_selector[:, None, :, None]
    key_part = jnp.einsum(
        "gled,edb->glb",
        masked[..., :rank_width],
        adapter_up_weight[:, 0],
        preferred_element_type=jnp.float32,
    )
    value_part = jnp.einsum(
        "gled,edb->glb",
        masked[..., rank_width:],
        adapter_up_weight[:, 1],
        preferred_element_type=jnp.float32,
    )
    delta_slots = jnp.stack([key_part, value_part], axis=2)
    delta_send = delta_slots.reshape(owner_count, cap * token_count * 2, column_count)
    delta_recv = lax.all_to_all(delta_send, "adapter", 0, 0, tiled=True)
    delta_rows = delta_recv.reshape(slot_total, token_count * 2 * column_count)
    adapter_update = jnp.take(delta_rows, slot_of, axis=0).reshape(
        row_count, token_count, 2, column_count
    )

    projected_output = base_proj + adapter_update
    positions = (cached_length[:, None] + jnp.arange(token_count, dtype=jnp.int32)[None, :]).astype(
        jnp.float32
    )
    kv_local = column_count // HEAD_DIM
    key_vecs = rotate_keys(
        projected_output[:, :, 0].reshape(row_count, token_count, kv_local, HEAD_DIM),
        positions[:, :, None],
    )
    new_keys = key_vecs.reshape(row_count, token_count, column_count).astype(jnp.bfloat16)
    new_values = projected_output[:, :, 1].astype(jnp.bfloat16)
    attended = attend(
        queries, cached_key_rows, cached_value_rows, cached_length, new_keys, new_values, HEAD_DIM
    )
    return (new_keys, new_values, attended)


def solution(mesh):
    in_specs = (
        P("adapter", None, None),
        P(),
        P(None, None, "tensor"),
        P("adapter", "tensor", None),
        P("adapter", None, None, "tensor"),
        P("adapter"),
        P("adapter", None, "tensor"),
        P("adapter", None, "tensor"),
        P("adapter", None, "tensor"),
        P("adapter"),
    )
    out_specs = (
        P("adapter", None, "tensor"),
        P("adapter", None, "tensor"),
        P("adapter", None, "tensor"),
    )
    return jax.shard_map(body, mesh=mesh, in_specs=in_specs, out_specs=out_specs, check_vma=False)
```

```python
import jax
import jax.numpy as jnp
from jax import lax
from jax.sharding import PartitionSpec as P

HEAD_DIM = 128
SLOT_CAPACITY = 6


epsilon = 1e-05
rope_base = 500000.0


def rotate_keys(key_vecs, positions):
    head_size = key_vecs.shape[-1]
    half_size = head_size // 2
    inverse = rope_base ** (-(jnp.arange(half_size, dtype=jnp.float32) * 2.0 / head_size))
    angles = positions[..., None] * inverse
    cosine = jnp.cos(angles)
    sine_part = jnp.sin(angles)
    first_half = key_vecs[..., :half_size]
    second = key_vecs[..., half_size:]
    return jnp.concatenate(
        [first_half * cosine - second * sine_part, second * cosine + first_half * sine_part],
        axis=-1,
    )


def normalize(hidden, input_norm_gain):
    values = hidden.astype(jnp.float32)
    meansq = jnp.mean(values * values, axis=-1, keepdims=True)
    return (values * lax.rsqrt(meansq + epsilon) * input_norm_gain.astype(jnp.float32)).astype(
        jnp.bfloat16
    )


def attend(
    queries, cached_key_rows, cached_value_rows, cached_length, new_keys, new_values, head_size
):
    row_total, token_total, query_width = queries.shape
    context = cached_key_rows.shape[1]
    kv_local = cached_key_rows.shape[2] // head_size
    group_size = query_width // (kv_local * head_size)
    score_scale = float(head_size) ** (-0.5)
    query_vecs = queries.reshape(row_total, token_total, kv_local, group_size, head_size)
    cache_vecs = cached_key_rows.reshape(row_total, context, kv_local, head_size)
    fresh_vecs = new_keys.reshape(row_total, token_total, kv_local, head_size)
    cache_scores = (
        jnp.einsum("rthgd,rjhd->rthgj", query_vecs, cache_vecs, preferred_element_type=jnp.float32)
        * score_scale
    )
    slot_live = jnp.arange(context, dtype=jnp.int32)[None, :] < cached_length[:, None]
    cache_scores = jnp.where(slot_live[:, None, None, None, :], cache_scores, -1e30)
    fresh_scores = (
        jnp.einsum("rthgd,rshd->rthgs", query_vecs, fresh_vecs, preferred_element_type=jnp.float32)
        * score_scale
    )
    causal = (
        jnp.arange(token_total, dtype=jnp.int32)[:, None]
        >= jnp.arange(token_total, dtype=jnp.int32)[None, :]
    )
    fresh_scores = jnp.where(causal[None, :, None, None, :], fresh_scores, -1e30)
    top_score = jnp.maximum(jnp.max(cache_scores, axis=-1), jnp.max(fresh_scores, axis=-1))[
        ..., None
    ]
    cache_weights = jnp.exp(cache_scores - top_score)
    fresh_weights = jnp.exp(fresh_scores - top_score)
    total_weight = jnp.sum(cache_weights, axis=-1, keepdims=True) + jnp.sum(
        fresh_weights, axis=-1, keepdims=True
    )
    cache_probs = (cache_weights / total_weight).astype(jnp.bfloat16)
    fresh_probs = (fresh_weights / total_weight).astype(jnp.bfloat16)
    cache_vals = cached_value_rows.reshape(row_total, context, kv_local, head_size)
    fresh_vals = new_values.reshape(row_total, token_total, kv_local, head_size)
    mixed_out = jnp.einsum(
        "rthgj,rjhd->rthgd", cache_probs, cache_vals, preferred_element_type=jnp.float32
    )
    mixed_out = mixed_out + jnp.einsum(
        "rthgs,rshd->rthgd", fresh_probs, fresh_vals, preferred_element_type=jnp.float32
    )
    return mixed_out.reshape(row_total, token_total, query_width).astype(jnp.bfloat16)


def body(
    hidden,
    input_norm_gain,
    key_value_weight,
    adapter_down_weight,
    adapter_up_weight,
    request_adapter,
    queries,
    cached_key_rows,
    cached_value_rows,
    cached_length,
):
    row_count, token_count, model_width = hidden.shape
    feature_total = adapter_down_weight.shape[1]
    adapter_number = adapter_down_weight.shape[0]
    rank_total = adapter_down_weight.shape[2]
    rank_width = adapter_up_weight.shape[2]
    column_count = key_value_weight.shape[2]
    owner_count = lax.axis_size("adapter")
    cap = SLOT_CAPACITY
    slot_total = owner_count * cap

    values = hidden.astype(jnp.float32)
    meansq = jnp.mean(values * values, axis=-1, keepdims=True)
    row_scale = lax.rsqrt(meansq + epsilon)
    normed_input = (values * row_scale * input_norm_gain.astype(jnp.float32)).astype(jnp.bfloat16)
    base_proj = jnp.dot(
        normed_input.reshape(row_count * token_count, model_width),
        key_value_weight.reshape(model_width, 2 * column_count),
        preferred_element_type=jnp.float32,
    )
    base_proj = lax.optimization_barrier(base_proj.reshape(row_count, token_count, 2, column_count))

    owner_of = request_adapter // adapter_number
    local_adapter = request_adapter - owner_of * adapter_number
    row_ids = jnp.arange(row_count, dtype=jnp.int32)
    same_owner = owner_of[:, None] == owner_of[None, :]
    earlier = row_ids[None, :] < row_ids[:, None]
    rank_in_owner = jnp.sum((same_owner & earlier).astype(jnp.int32), axis=1)
    slot_of = owner_of * cap + rank_in_owner
    pick = (slot_of[None, :] == jnp.arange(slot_total, dtype=jnp.int32)[:, None]).astype(
        jnp.bfloat16
    )

    feature_start = lax.axis_index("tensor") * feature_total
    hidden_shard = lax.dynamic_slice_in_dim(hidden, feature_start, feature_total, 2)
    gain_shard = lax.dynamic_slice_in_dim(input_norm_gain, feature_start, feature_total, 0)
    own_features = (
        hidden_shard.astype(jnp.float32) * row_scale * gain_shard.astype(jnp.float32)
    ).astype(jnp.bfloat16)
    packed = jnp.dot(
        pick,
        own_features.reshape(row_count, token_count * feature_total),
        preferred_element_type=jnp.float32,
    ).astype(jnp.bfloat16)
    packed = packed.reshape(owner_count, cap * token_count, feature_total)
    slot_adapter = jnp.dot(
        pick, local_adapter.astype(jnp.bfloat16), preferred_element_type=jnp.float32
    ).astype(jnp.bfloat16)
    id_row = jnp.zeros((owner_count, 1, feature_total), jnp.bfloat16)
    id_row = lax.dynamic_update_slice(
        id_row, slot_adapter.reshape(owner_count, 1, cap), (0, 0, 0)
    )
    send = jnp.concatenate([packed, id_row], axis=1)
    recv = lax.all_to_all(send, "adapter", 0, 0, tiled=True)

    got_rows = recv[:, : cap * token_count].reshape(slot_total, token_count, feature_total)
    got_adapter = recv[:, cap * token_count, :cap].reshape(slot_total).astype(jnp.int32)
    selector = (
        got_adapter[:, None] == jnp.arange(adapter_number, dtype=jnp.int32)[None, :]
    ).astype(jnp.float32)

    down_all = jnp.einsum(
        "euz,nzs->euns", got_rows, adapter_down_weight, preferred_element_type=jnp.float32
    )
    partial_rank = jnp.sum(down_all * selector[:, None, :, None], axis=2)
    every_partial = lax.all_gather(partial_rank, "tensor", axis=0, tiled=False)
    rank_hidden = jnp.sum(every_partial, axis=0).astype(jnp.bfloat16)

    rank_selector = selector.astype(jnp.bfloat16)
    masked = rank_hidden[:, :, None, :] * rank_selector[:, None, :, None]
    key_part = jnp.einsum(
        "gled,edb->glb",
        masked[..., :rank_width],
        adapter_up_weight[:, 0],
        preferred_element_type=jnp.float32,
    )
    value_part = jnp.einsum(
        "gled,edb->glb",
        masked[..., rank_width:],
        adapter_up_weight[:, 1],
        preferred_element_type=jnp.float32,
    )
    delta_slots = jnp.stack([key_part, value_part], axis=2)
    delta_send = delta_slots.reshape(owner_count, cap * token_count * 2, column_count)
    delta_recv = lax.all_to_all(delta_send, "adapter", 0, 0, tiled=True)
    delta_rows = delta_recv.reshape(slot_total, token_count * 2 * column_count)
    adapter_update = jnp.take(delta_rows, slot_of, axis=0).reshape(
        row_count, token_count, 2, column_count
    )

    projected_output = base_proj + adapter_update
    positions = (cached_length[:, None] + jnp.arange(token_count, dtype=jnp.int32)[None, :]).astype(
        jnp.float32
    )
    kv_local = column_count // HEAD_DIM
    key_vecs = rotate_keys(
        projected_output[:, :, 0].reshape(row_count, token_count, kv_local, HEAD_DIM),
        positions[:, :, None],
    )
    new_keys = key_vecs.reshape(row_count, token_count, column_count).astype(jnp.bfloat16)
    new_values = projected_output[:, :, 1].astype(jnp.bfloat16)
    attended = attend(
        queries, cached_key_rows, cached_value_rows, cached_length, new_keys, new_values, HEAD_DIM
    )
    return (new_keys, new_values, attended)


def solution(mesh):
    in_specs = (
        P("adapter", None, None),
        P(),
        P(None, None, "tensor"),
        P("adapter", "tensor", None),
        P("adapter", None, None, "tensor"),
        P("adapter"),
        P("adapter", None, "tensor"),
        P("adapter", None, "tensor"),
        P("adapter", None, "tensor"),
        P("adapter"),
    )
    out_specs = (
        P("adapter", None, "tensor"),
        P("adapter", None, "tensor"),
        P("adapter", None, "tensor"),
    )
    return jax.shard_map(body, mesh=mesh, in_specs=in_specs, out_specs=out_specs, check_vma=False)
```

```python
import jax
import jax.numpy as jnp
from jax import lax
from jax.sharding import PartitionSpec as P

HEAD_DIM = 128
SLOT_CAPACITY = 6


epsilon = 1e-05
rope_base = 500000.0


def rotate_keys(key_vecs, positions):
    head_size = key_vecs.shape[-1]
    half_size = head_size // 2
    inverse = rope_base ** (-(jnp.arange(half_size, dtype=jnp.float32) * 2.0 / head_size))
    angles = positions[..., None] * inverse
    cosine = jnp.cos(angles)
    sine_part = jnp.sin(angles)
    first_half = key_vecs[..., :half_size]
    second = key_vecs[..., half_size:]
    return jnp.concatenate(
        [first_half * cosine - second * sine_part, second * cosine + first_half * sine_part],
        axis=-1,
    )


def normalize(hidden, input_norm_gain):
    values = hidden.astype(jnp.float32)
    meansq = jnp.mean(values * values, axis=-1, keepdims=True)
    return (values * lax.rsqrt(meansq + epsilon) * input_norm_gain.astype(jnp.float32)).astype(
        jnp.bfloat16
    )


def attend(
    queries, cached_key_rows, cached_value_rows, cached_length, new_keys, new_values, head_size
):
    row_total, token_total, query_width = queries.shape
    context = cached_key_rows.shape[1]
    kv_local = cached_key_rows.shape[2] // head_size
    group_size = query_width // (kv_local * head_size)
    score_scale = float(head_size) ** (-0.5)
    query_vecs = queries.reshape(row_total, token_total, kv_local, group_size, head_size)
    cache_vecs = cached_key_rows.reshape(row_total, context, kv_local, head_size)
    fresh_vecs = new_keys.reshape(row_total, token_total, kv_local, head_size)
    cache_scores = (
        jnp.einsum("rthgd,rjhd->rthgj", query_vecs, cache_vecs, preferred_element_type=jnp.float32)
        * score_scale
    )
    slot_live = jnp.arange(context, dtype=jnp.int32)[None, :] < cached_length[:, None]
    cache_scores = jnp.where(slot_live[:, None, None, None, :], cache_scores, -1e30)
    fresh_scores = (
        jnp.einsum("rthgd,rshd->rthgs", query_vecs, fresh_vecs, preferred_element_type=jnp.float32)
        * score_scale
    )
    causal = (
        jnp.arange(token_total, dtype=jnp.int32)[:, None]
        >= jnp.arange(token_total, dtype=jnp.int32)[None, :]
    )
    fresh_scores = jnp.where(causal[None, :, None, None, :], fresh_scores, -1e30)
    top_score = jnp.maximum(jnp.max(cache_scores, axis=-1), jnp.max(fresh_scores, axis=-1))[
        ..., None
    ]
    cache_weights = jnp.exp(cache_scores - top_score)
    fresh_weights = jnp.exp(fresh_scores - top_score)
    total_weight = jnp.sum(cache_weights, axis=-1, keepdims=True) + jnp.sum(
        fresh_weights, axis=-1, keepdims=True
    )
    cache_probs = (cache_weights / total_weight).astype(jnp.bfloat16)
    fresh_probs = (fresh_weights / total_weight).astype(jnp.bfloat16)
    cache_vals = cached_value_rows.reshape(row_total, context, kv_local, head_size)
    fresh_vals = new_values.reshape(row_total, token_total, kv_local, head_size)
    mixed_out = jnp.einsum(
        "rthgj,rjhd->rthgd", cache_probs, cache_vals, preferred_element_type=jnp.float32
    )
    mixed_out = mixed_out + jnp.einsum(
        "rthgs,rshd->rthgd", fresh_probs, fresh_vals, preferred_element_type=jnp.float32
    )
    return mixed_out.reshape(row_total, token_total, query_width).astype(jnp.bfloat16)


def body(
    hidden,
    input_norm_gain,
    key_value_weight,
    adapter_down_weight,
    adapter_up_weight,
    request_adapter,
    queries,
    cached_key_rows,
    cached_value_rows,
    cached_length,
):
    row_count, token_count, model_width = hidden.shape
    feature_total = adapter_down_weight.shape[1]
    adapter_number = adapter_down_weight.shape[0]
    rank_total = adapter_down_weight.shape[2]
    rank_width = adapter_up_weight.shape[2]
    column_count = key_value_weight.shape[2]
    owner_count = lax.axis_size("adapter")
    cap = SLOT_CAPACITY
    slot_total = owner_count * cap

    values = hidden.astype(jnp.float32)
    meansq = jnp.mean(values * values, axis=-1, keepdims=True)
    row_scale = lax.rsqrt(meansq + epsilon)
    normed_input = (values * row_scale * input_norm_gain.astype(jnp.float32)).astype(jnp.bfloat16)
    base_proj = jnp.dot(
        normed_input.reshape(row_count * token_count, model_width),
        key_value_weight.reshape(model_width, 2 * column_count),
        preferred_element_type=jnp.float32,
    )
    base_proj = lax.optimization_barrier(base_proj.reshape(row_count, token_count, 2, column_count))

    owner_of = request_adapter // adapter_number
    local_adapter = request_adapter - owner_of * adapter_number
    row_ids = jnp.arange(row_count, dtype=jnp.int32)
    same_owner = owner_of[:, None] == owner_of[None, :]
    earlier = row_ids[None, :] < row_ids[:, None]
    rank_in_owner = jnp.sum((same_owner & earlier).astype(jnp.int32), axis=1)
    slot_of = owner_of * cap + rank_in_owner
    pick = (slot_of[None, :] == jnp.arange(slot_total, dtype=jnp.int32)[:, None]).astype(
        jnp.bfloat16
    )

    feature_start = lax.axis_index("tensor") * feature_total
    hidden_shard = lax.dynamic_slice_in_dim(hidden, feature_start, feature_total, 2)
    gain_shard = lax.dynamic_slice_in_dim(input_norm_gain, feature_start, feature_total, 0)
    own_features = (
        hidden_shard.astype(jnp.float32) * row_scale * gain_shard.astype(jnp.float32)
    ).astype(jnp.bfloat16)
    packed = jnp.dot(
        pick,
        own_features.reshape(row_count, token_count * feature_total),
        preferred_element_type=jnp.float32,
    ).astype(jnp.bfloat16)
    packed = packed.reshape(owner_count, cap * token_count, feature_total)
    slot_adapter = jnp.dot(
        pick, local_adapter.astype(jnp.bfloat16), preferred_element_type=jnp.float32
    ).astype(jnp.bfloat16)
    id_row = jnp.zeros((owner_count, 1, feature_total), jnp.bfloat16)
    id_row = lax.dynamic_update_slice(
        id_row, slot_adapter.reshape(owner_count, 1, cap), (0, 0, 0)
    )
    send = jnp.concatenate([packed, id_row], axis=1)
    recv = lax.all_to_all(send, "adapter", 0, 0, tiled=True)

    got_rows = recv[:, : cap * token_count].reshape(slot_total, token_count, feature_total)
    got_adapter = recv[:, cap * token_count, :cap].reshape(slot_total).astype(jnp.int32)
    selector = (
        got_adapter[:, None] == jnp.arange(adapter_number, dtype=jnp.int32)[None, :]
    ).astype(jnp.float32)

    down_all = jnp.einsum(
        "euz,nzs->euns", got_rows, adapter_down_weight, preferred_element_type=jnp.float32
    )
    partial_rank = jnp.sum(down_all * selector[:, None, :, None], axis=2)
    rank_hidden = lax.psum(partial_rank, "tensor").astype(jnp.bfloat16)

    rank_selector = selector.astype(jnp.bfloat16)
    masked = rank_hidden[:, :, None, :] * rank_selector[:, None, :, None]
    key_part = jnp.einsum(
        "gled,edb->glb",
        masked[..., :rank_width],
        adapter_up_weight[:, 0],
        preferred_element_type=jnp.float32,
    )
    value_part = jnp.einsum(
        "gled,edb->glb",
        masked[..., rank_width:],
        adapter_up_weight[:, 1],
        preferred_element_type=jnp.float32,
    )
    delta_slots = jnp.stack([key_part, value_part], axis=2)
    delta_send = delta_slots.reshape(owner_count, cap * token_count * 2, column_count)
    delta_recv = lax.all_to_all(delta_send.astype(jnp.bfloat16), "adapter", 0, 0, tiled=True)
    delta_rows = delta_recv.reshape(slot_total, token_count * 2 * column_count).astype(jnp.float32)
    adapter_update = jnp.take(delta_rows, slot_of, axis=0).reshape(
        row_count, token_count, 2, column_count
    )

    projected_output = base_proj + adapter_update
    positions = (cached_length[:, None] + jnp.arange(token_count, dtype=jnp.int32)[None, :]).astype(
        jnp.float32
    )
    kv_local = column_count // HEAD_DIM
    key_vecs = rotate_keys(
        projected_output[:, :, 0].reshape(row_count, token_count, kv_local, HEAD_DIM),
        positions[:, :, None],
    )
    new_keys = key_vecs.reshape(row_count, token_count, column_count).astype(jnp.bfloat16)
    new_values = projected_output[:, :, 1].astype(jnp.bfloat16)
    attended = attend(
        queries, cached_key_rows, cached_value_rows, cached_length, new_keys, new_values, HEAD_DIM
    )
    return (new_keys, new_values, attended)


def solution(mesh):
    in_specs = (
        P("adapter", None, None),
        P(),
        P(None, None, "tensor"),
        P("adapter", "tensor", None),
        P("adapter", None, None, "tensor"),
        P("adapter"),
        P("adapter", None, "tensor"),
        P("adapter", None, "tensor"),
        P("adapter", None, "tensor"),
        P("adapter"),
    )
    out_specs = (
        P("adapter", None, "tensor"),
        P("adapter", None, "tensor"),
        P("adapter", None, "tensor"),
    )
    return jax.shard_map(body, mesh=mesh, in_specs=in_specs, out_specs=out_specs, check_vma=False)
```

```python
import jax
import jax.numpy as jnp
from jax import lax
from jax.sharding import Mesh, PartitionSpec as P

HEAD_DIM = 128
SLOT_CAPACITY = 6


epsilon = 1e-05
rope_base = 500000.0


def rotate_keys(key_vecs, positions):
    head_size = key_vecs.shape[-1]
    half_size = head_size // 2
    inverse = rope_base ** (-(jnp.arange(half_size, dtype=jnp.float32) * 2.0 / head_size))
    angles = positions[..., None] * inverse
    cosine = jnp.cos(angles)
    sine_part = jnp.sin(angles)
    first_half = key_vecs[..., :half_size]
    second = key_vecs[..., half_size:]
    return jnp.concatenate(
        [first_half * cosine - second * sine_part, second * cosine + first_half * sine_part],
        axis=-1,
    )


def normalize(hidden, input_norm_gain):
    values = hidden.astype(jnp.float32)
    meansq = jnp.mean(values * values, axis=-1, keepdims=True)
    return (values * lax.rsqrt(meansq + epsilon) * input_norm_gain.astype(jnp.float32)).astype(
        jnp.bfloat16
    )


def attend(
    queries, cached_key_rows, cached_value_rows, cached_length, new_keys, new_values, head_size
):
    row_total, token_total, query_width = queries.shape
    context = cached_key_rows.shape[1]
    kv_local = cached_key_rows.shape[2] // head_size
    group_size = query_width // (kv_local * head_size)
    score_scale = float(head_size) ** (-0.5)
    query_vecs = queries.reshape(row_total, token_total, kv_local, group_size, head_size)
    cache_vecs = cached_key_rows.reshape(row_total, context, kv_local, head_size)
    fresh_vecs = new_keys.reshape(row_total, token_total, kv_local, head_size)
    cache_scores = (
        jnp.einsum("rthgd,rjhd->rthgj", query_vecs, cache_vecs, preferred_element_type=jnp.float32)
        * score_scale
    )
    slot_live = jnp.arange(context, dtype=jnp.int32)[None, :] < cached_length[:, None]
    cache_scores = jnp.where(slot_live[:, None, None, None, :], cache_scores, -1e30)
    fresh_scores = (
        jnp.einsum("rthgd,rshd->rthgs", query_vecs, fresh_vecs, preferred_element_type=jnp.float32)
        * score_scale
    )
    causal = (
        jnp.arange(token_total, dtype=jnp.int32)[:, None]
        >= jnp.arange(token_total, dtype=jnp.int32)[None, :]
    )
    fresh_scores = jnp.where(causal[None, :, None, None, :], fresh_scores, -1e30)
    top_score = jnp.maximum(jnp.max(cache_scores, axis=-1), jnp.max(fresh_scores, axis=-1))[
        ..., None
    ]
    cache_weights = jnp.exp(cache_scores - top_score)
    fresh_weights = jnp.exp(fresh_scores - top_score)
    total_weight = jnp.sum(cache_weights, axis=-1, keepdims=True) + jnp.sum(
        fresh_weights, axis=-1, keepdims=True
    )
    cache_probs = (cache_weights / total_weight).astype(jnp.bfloat16)
    fresh_probs = (fresh_weights / total_weight).astype(jnp.bfloat16)
    cache_vals = cached_value_rows.reshape(row_total, context, kv_local, head_size)
    fresh_vals = new_values.reshape(row_total, token_total, kv_local, head_size)
    mixed_out = jnp.einsum(
        "rthgj,rjhd->rthgd", cache_probs, cache_vals, preferred_element_type=jnp.float32
    )
    mixed_out = mixed_out + jnp.einsum(
        "rthgs,rshd->rthgd", fresh_probs, fresh_vals, preferred_element_type=jnp.float32
    )
    return mixed_out.reshape(row_total, token_total, query_width).astype(jnp.bfloat16)


def body(
    hidden,
    input_norm_gain,
    key_value_weight,
    adapter_down_weight,
    adapter_up_weight,
    request_adapter,
    queries,
    cached_key_rows,
    cached_value_rows,
    cached_length,
):
    row_count, token_count, model_width = hidden.shape
    feature_total = adapter_down_weight.shape[1]
    adapter_number = adapter_down_weight.shape[0]
    rank_total = adapter_down_weight.shape[2]
    rank_width = adapter_up_weight.shape[2]
    column_count = key_value_weight.shape[2]
    owner_count = lax.axis_size("adapter")
    cap = SLOT_CAPACITY
    slot_total = owner_count * cap

    values = hidden.astype(jnp.float32)
    meansq = jnp.mean(values * values, axis=-1, keepdims=True)
    row_scale = lax.rsqrt(meansq + epsilon)
    normed_input = (values * row_scale * input_norm_gain.astype(jnp.float32)).astype(jnp.bfloat16)
    base_proj = jnp.dot(
        normed_input.reshape(row_count * token_count, model_width),
        key_value_weight.reshape(model_width, 2 * column_count),
        preferred_element_type=jnp.float32,
    )
    base_proj = lax.optimization_barrier(base_proj.reshape(row_count, token_count, 2, column_count))

    owner_of = request_adapter // adapter_number
    local_adapter = request_adapter - owner_of * adapter_number
    row_ids = jnp.arange(row_count, dtype=jnp.int32)
    same_owner = owner_of[:, None] == owner_of[None, :]
    earlier = row_ids[None, :] < row_ids[:, None]
    rank_in_owner = jnp.sum((same_owner & earlier).astype(jnp.int32), axis=1)
    slot_of = owner_of * cap + rank_in_owner
    pick = (slot_of[None, :] == jnp.arange(slot_total, dtype=jnp.int32)[:, None]).astype(
        jnp.bfloat16
    )

    feature_start = (lax.axis_index("tx") * lax.axis_size("tc") + lax.axis_index("tc")) * feature_total
    hidden_shard = lax.dynamic_slice_in_dim(hidden, feature_start, feature_total, 2)
    gain_shard = lax.dynamic_slice_in_dim(input_norm_gain, feature_start, feature_total, 0)
    own_features = (
        hidden_shard.astype(jnp.float32) * row_scale * gain_shard.astype(jnp.float32)
    ).astype(jnp.bfloat16)
    packed = jnp.dot(
        pick,
        own_features.reshape(row_count, token_count * feature_total),
        preferred_element_type=jnp.float32,
    ).astype(jnp.bfloat16)
    packed = packed.reshape(owner_count, cap * token_count, feature_total)
    slot_adapter = jnp.dot(
        pick, local_adapter.astype(jnp.bfloat16), preferred_element_type=jnp.float32
    ).astype(jnp.bfloat16)
    id_row = jnp.zeros((owner_count, 1, feature_total), jnp.bfloat16)
    id_row = lax.dynamic_update_slice(
        id_row, slot_adapter.reshape(owner_count, 1, cap), (0, 0, 0)
    )
    send = jnp.concatenate([packed, id_row], axis=1)
    recv = lax.all_to_all(send, "adapter", 0, 0, tiled=True)

    got_rows = recv[:, : cap * token_count].reshape(slot_total, token_count, feature_total)
    got_adapter = recv[:, cap * token_count, :cap].reshape(slot_total).astype(jnp.int32)
    selector = (
        got_adapter[:, None] == jnp.arange(adapter_number, dtype=jnp.int32)[None, :]
    ).astype(jnp.float32)

    down_all = jnp.einsum(
        "euz,nzs->euns", got_rows, adapter_down_weight, preferred_element_type=jnp.float32
    )
    partial_rank = jnp.sum(down_all * selector[:, None, :, None], axis=2)
    rank_hidden = lax.psum(lax.psum(partial_rank, "tc"), "tx").astype(jnp.bfloat16)

    rank_selector = selector.astype(jnp.bfloat16)
    masked = rank_hidden[:, :, None, :] * rank_selector[:, None, :, None]
    key_part = jnp.einsum(
        "gled,edb->glb",
        masked[..., :rank_width],
        adapter_up_weight[:, 0],
        preferred_element_type=jnp.float32,
    )
    value_part = jnp.einsum(
        "gled,edb->glb",
        masked[..., rank_width:],
        adapter_up_weight[:, 1],
        preferred_element_type=jnp.float32,
    )
    delta_slots = jnp.stack([key_part, value_part], axis=2)
    delta_send = delta_slots.reshape(owner_count, cap * token_count * 2, column_count)
    delta_recv = lax.all_to_all(delta_send, "adapter", 0, 0, tiled=True)
    delta_rows = delta_recv.reshape(slot_total, token_count * 2 * column_count)
    adapter_update = jnp.take(delta_rows, slot_of, axis=0).reshape(
        row_count, token_count, 2, column_count
    )

    projected_output = base_proj + adapter_update
    positions = (cached_length[:, None] + jnp.arange(token_count, dtype=jnp.int32)[None, :]).astype(
        jnp.float32
    )
    kv_local = column_count // HEAD_DIM
    key_vecs = rotate_keys(
        projected_output[:, :, 0].reshape(row_count, token_count, kv_local, HEAD_DIM),
        positions[:, :, None],
    )
    new_keys = key_vecs.reshape(row_count, token_count, column_count).astype(jnp.bfloat16)
    new_values = projected_output[:, :, 1].astype(jnp.bfloat16)
    attended = attend(
        queries, cached_key_rows, cached_value_rows, cached_length, new_keys, new_values, HEAD_DIM
    )
    return (new_keys, new_values, attended)


def solution(mesh):
    tensor_devices = mesh.devices.shape[1]
    core_count = 2 if tensor_devices % 2 == 0 else 1
    split_mesh = Mesh(
        mesh.devices.reshape(mesh.devices.shape[0], tensor_devices // core_count, core_count),
        ("adapter", "tx", "tc"),
    )
    tensor = ("tx", "tc")
    in_specs = (
        P("adapter", None, None),
        P(),
        P(None, None, tensor),
        P("adapter", tensor, None),
        P("adapter", None, None, tensor),
        P("adapter"),
        P("adapter", None, tensor),
        P("adapter", None, tensor),
        P("adapter", None, tensor),
        P("adapter"),
    )
    out_specs = (
        P("adapter", None, tensor),
        P("adapter", None, tensor),
        P("adapter", None, tensor),
    )
    return jax.shard_map(
        body, mesh=split_mesh, in_specs=in_specs, out_specs=out_specs, check_vma=False
    )
```

```python
import jax
import jax.numpy as jnp
from jax import lax
from jax.sharding import PartitionSpec as P

HEAD_DIM = 128
SLOT_CAPACITY = 6


epsilon = 1e-05
rope_base = 500000.0


def rotate_keys(key_vecs, positions):
    head_size = key_vecs.shape[-1]
    half_size = head_size // 2
    inverse = rope_base ** (-(jnp.arange(half_size, dtype=jnp.float32) * 2.0 / head_size))
    angles = positions[..., None] * inverse
    cosine = jnp.cos(angles)
    sine_part = jnp.sin(angles)
    first_half = key_vecs[..., :half_size]
    second = key_vecs[..., half_size:]
    return jnp.concatenate(
        [first_half * cosine - second * sine_part, second * cosine + first_half * sine_part],
        axis=-1,
    )


def normalize(hidden, input_norm_gain):
    values = hidden.astype(jnp.float32)
    square_grid = jnp.einsum("rtd,sud->rtsu", hidden, hidden, preferred_element_type=jnp.float32)
    row_index = jnp.arange(row_count, dtype=jnp.int32)
    token_index = jnp.arange(token_count, dtype=jnp.int32)
    diagonal = (row_index[:, None, None, None] == row_index[None, None, :, None]) & (
        token_index[None, :, None, None] == token_index[None, None, None, :]
    )
    meansq = (
        jnp.sum(jnp.where(diagonal, square_grid, 0.0), axis=(2, 3))[..., None] / model_width
    )
    return (values * lax.rsqrt(meansq + epsilon) * input_norm_gain.astype(jnp.float32)).astype(
        jnp.bfloat16
    )


def attend(
    queries, cached_key_rows, cached_value_rows, cached_length, new_keys, new_values, head_size
):
    row_total, token_total, query_width = queries.shape
    context = cached_key_rows.shape[1]
    kv_local = cached_key_rows.shape[2] // head_size
    group_size = query_width // (kv_local * head_size)
    score_scale = float(head_size) ** (-0.5)
    query_vecs = queries.reshape(row_total, token_total, kv_local, group_size, head_size)
    cache_vecs = cached_key_rows.reshape(row_total, context, kv_local, head_size)
    fresh_vecs = new_keys.reshape(row_total, token_total, kv_local, head_size)
    cache_scores = (
        jnp.einsum("rthgd,rjhd->rthgj", query_vecs, cache_vecs, preferred_element_type=jnp.float32)
        * score_scale
    )
    slot_live = jnp.arange(context, dtype=jnp.int32)[None, :] < cached_length[:, None]
    cache_scores = jnp.where(slot_live[:, None, None, None, :], cache_scores, -1e30)
    fresh_scores = (
        jnp.sum(
            query_vecs.astype(jnp.float32)[:, :, :, :, None, :]
            * jnp.moveaxis(fresh_vecs.astype(jnp.float32), 1, 2)[:, None, :, None, :, :],
            axis=-1,
        )
        * score_scale
    )
    causal = (
        jnp.arange(token_total, dtype=jnp.int32)[:, None]
        >= jnp.arange(token_total, dtype=jnp.int32)[None, :]
    )
    fresh_scores = jnp.where(causal[None, :, None, None, :], fresh_scores, -1e30)
    top_score = jnp.maximum(jnp.max(cache_scores, axis=-1), jnp.max(fresh_scores, axis=-1))[
        ..., None
    ]
    cache_weights = jnp.exp(cache_scores - top_score)
    fresh_weights = jnp.exp(fresh_scores - top_score)
    total_weight = jnp.sum(cache_weights, axis=-1, keepdims=True) + jnp.sum(
        fresh_weights, axis=-1, keepdims=True
    )
    cache_probs = (cache_weights / total_weight).astype(jnp.bfloat16)
    fresh_probs = (fresh_weights / total_weight).astype(jnp.bfloat16)
    cache_vals = cached_value_rows.reshape(row_total, context, kv_local, head_size)
    fresh_vals = new_values.reshape(row_total, token_total, kv_local, head_size)
    mixed_out = jnp.einsum(
        "rthgj,rjhd->rthgd", cache_probs, cache_vals, preferred_element_type=jnp.float32
    )
    mixed_out = mixed_out + jnp.einsum(
        "rthgs,rshd->rthgd", fresh_probs, fresh_vals, preferred_element_type=jnp.float32
    )
    return mixed_out.reshape(row_total, token_total, query_width).astype(jnp.bfloat16)


def body(
    hidden,
    input_norm_gain,
    key_value_weight,
    adapter_down_weight,
    adapter_up_weight,
    request_adapter,
    queries,
    cached_key_rows,
    cached_value_rows,
    cached_length,
):
    row_count, token_count, model_width = hidden.shape
    feature_total = adapter_down_weight.shape[1]
    adapter_number = adapter_down_weight.shape[0]
    rank_total = adapter_down_weight.shape[2]
    rank_width = adapter_up_weight.shape[2]
    column_count = key_value_weight.shape[2]
    owner_count = lax.axis_size("adapter")
    cap = SLOT_CAPACITY
    slot_total = owner_count * cap

    values = hidden.astype(jnp.float32)
    square_grid = jnp.einsum("rtd,sud->rtsu", hidden, hidden, preferred_element_type=jnp.float32)
    row_index = jnp.arange(row_count, dtype=jnp.int32)
    token_index = jnp.arange(token_count, dtype=jnp.int32)
    diagonal = (row_index[:, None, None, None] == row_index[None, None, :, None]) & (
        token_index[None, :, None, None] == token_index[None, None, None, :]
    )
    meansq = (
        jnp.sum(jnp.where(diagonal, square_grid, 0.0), axis=(2, 3))[..., None] / model_width
    )
    row_scale = lax.rsqrt(meansq + epsilon)
    normed_input = (values * row_scale * input_norm_gain.astype(jnp.float32)).astype(jnp.bfloat16)
    base_proj = jnp.dot(
        normed_input.reshape(row_count * token_count, model_width),
        key_value_weight.reshape(model_width, 2 * column_count),
        preferred_element_type=jnp.float32,
    )
    base_proj = lax.optimization_barrier(base_proj.reshape(row_count, token_count, 2, column_count))

    owner_of = request_adapter // adapter_number
    local_adapter = request_adapter - owner_of * adapter_number
    row_ids = jnp.arange(row_count, dtype=jnp.int32)
    same_owner = owner_of[:, None] == owner_of[None, :]
    earlier = row_ids[None, :] < row_ids[:, None]
    rank_in_owner = jnp.sum((same_owner & earlier).astype(jnp.int32), axis=1)
    slot_of = owner_of * cap + rank_in_owner
    pick = (slot_of[None, :] == jnp.arange(slot_total, dtype=jnp.int32)[:, None]).astype(
        jnp.bfloat16
    )

    feature_start = lax.axis_index("tensor") * feature_total
    hidden_shard = lax.dynamic_slice_in_dim(hidden, feature_start, feature_total, 2)
    gain_shard = lax.dynamic_slice_in_dim(input_norm_gain, feature_start, feature_total, 0)
    own_features = (
        hidden_shard.astype(jnp.float32) * row_scale * gain_shard.astype(jnp.float32)
    ).astype(jnp.bfloat16)
    packed = jnp.dot(
        pick,
        own_features.reshape(row_count, token_count * feature_total),
        preferred_element_type=jnp.float32,
    ).astype(jnp.bfloat16)
    packed = packed.reshape(owner_count, cap * token_count, feature_total)
    slot_adapter = jnp.dot(
        pick, local_adapter.astype(jnp.bfloat16), preferred_element_type=jnp.float32
    ).astype(jnp.bfloat16)
    id_row = jnp.zeros((owner_count, 1, feature_total), jnp.bfloat16)
    id_row = lax.dynamic_update_slice(
        id_row, slot_adapter.reshape(owner_count, 1, cap), (0, 0, 0)
    )
    send = jnp.concatenate([packed, id_row], axis=1)
    recv = lax.all_to_all(send, "adapter", 0, 0, tiled=True)

    got_rows = recv[:, : cap * token_count].reshape(slot_total, token_count, feature_total)
    got_adapter = recv[:, cap * token_count, :cap].reshape(slot_total).astype(jnp.int32)
    selector = (
        got_adapter[:, None] == jnp.arange(adapter_number, dtype=jnp.int32)[None, :]
    ).astype(jnp.float32)

    down_all = jnp.einsum(
        "euz,nzs->euns", got_rows, adapter_down_weight, preferred_element_type=jnp.float32
    )
    partial_rank = jnp.sum(down_all * selector[:, None, :, None], axis=2)
    rank_hidden = lax.psum(partial_rank, "tensor").astype(jnp.bfloat16)

    rank_selector = selector.astype(jnp.bfloat16)
    masked = rank_hidden[:, :, None, :] * rank_selector[:, None, :, None]
    key_part = jnp.einsum(
        "gled,edb->glb",
        masked[..., :rank_width],
        adapter_up_weight[:, 0],
        preferred_element_type=jnp.float32,
    )
    value_part = jnp.einsum(
        "gled,edb->glb",
        masked[..., rank_width:],
        adapter_up_weight[:, 1],
        preferred_element_type=jnp.float32,
    )
    delta_slots = jnp.stack([key_part, value_part], axis=2)
    delta_send = delta_slots.reshape(owner_count, cap * token_count * 2, column_count)
    delta_recv = lax.all_to_all(delta_send, "adapter", 0, 0, tiled=True)
    delta_rows = delta_recv.reshape(slot_total, token_count * 2 * column_count)
    adapter_update = jnp.take(delta_rows, slot_of, axis=0).reshape(
        row_count, token_count, 2, column_count
    )

    projected_output = base_proj + adapter_update
    positions = (cached_length[:, None] + jnp.arange(token_count, dtype=jnp.int32)[None, :]).astype(
        jnp.float32
    )
    kv_local = column_count // HEAD_DIM
    key_vecs = rotate_keys(
        projected_output[:, :, 0].reshape(row_count, token_count, kv_local, HEAD_DIM),
        positions[:, :, None],
    )
    new_keys = key_vecs.reshape(row_count, token_count, column_count).astype(jnp.bfloat16)
    new_values = projected_output[:, :, 1].astype(jnp.bfloat16)
    attended = attend(
        queries, cached_key_rows, cached_value_rows, cached_length, new_keys, new_values, HEAD_DIM
    )
    return (new_keys, new_values, attended)


def solution(mesh):
    in_specs = (
        P("adapter", None, None),
        P(),
        P(None, None, "tensor"),
        P("adapter", "tensor", None),
        P("adapter", None, None, "tensor"),
        P("adapter"),
        P("adapter", None, "tensor"),
        P("adapter", None, "tensor"),
        P("adapter", None, "tensor"),
        P("adapter"),
    )
    out_specs = (
        P("adapter", None, "tensor"),
        P("adapter", None, "tensor"),
        P("adapter", None, "tensor"),
    )
    return jax.shard_map(body, mesh=mesh, in_specs=in_specs, out_specs=out_specs, check_vma=False)
```

```python
import jax
import jax.numpy as jnp
from jax import lax
from jax.sharding import PartitionSpec as P

HEAD_DIM = 128
SLOT_CAPACITY = 6


epsilon = 1e-05
rope_base = 500000.0


def rotate_keys(key_vecs, positions):
    head_size = key_vecs.shape[-1]
    half_size = head_size // 2
    inverse = rope_base ** (-(jnp.arange(half_size, dtype=jnp.float32) * 2.0 / head_size))
    angles = positions[..., None] * inverse
    cosine = jnp.cos(angles)
    sine_part = jnp.sin(angles)
    first_half = key_vecs[..., :half_size]
    second = key_vecs[..., half_size:]
    return jnp.concatenate(
        [first_half * cosine - second * sine_part, second * cosine + first_half * sine_part],
        axis=-1,
    )


def normalize(hidden, input_norm_gain):
    values = hidden.astype(jnp.float32)
    meansq = jnp.mean(values * values, axis=-1, keepdims=True)
    return (values * lax.rsqrt(meansq + epsilon) * input_norm_gain.astype(jnp.float32)).astype(
        jnp.bfloat16
    )


def attend(
    queries, cached_key_rows, cached_value_rows, cached_length, new_keys, new_values, head_size
):
    row_total, token_total, query_width = queries.shape
    context = cached_key_rows.shape[1]
    kv_local = cached_key_rows.shape[2] // head_size
    group_size = query_width // (kv_local * head_size)
    score_scale = float(head_size) ** (-0.5)
    query_vecs = queries.reshape(row_total, token_total, kv_local, group_size, head_size)
    cache_vecs = cached_key_rows.reshape(row_total, context, kv_local, head_size)
    fresh_vecs = new_keys.reshape(row_total, token_total, kv_local, head_size)
    cache_scores = (
        jnp.einsum("rthgd,rjhd->rthgj", query_vecs, cache_vecs, preferred_element_type=jnp.float32)
        * score_scale
    )
    slot_live = jnp.arange(context, dtype=jnp.int32)[None, :] < cached_length[:, None]
    cache_scores = jnp.where(slot_live[:, None, None, None, :], cache_scores, -1e30)
    fresh_scores = (
        jnp.einsum("rthgd,rshd->rthgs", query_vecs, fresh_vecs, preferred_element_type=jnp.float32)
        * score_scale
    )
    causal = (
        jnp.arange(token_total, dtype=jnp.int32)[:, None]
        >= jnp.arange(token_total, dtype=jnp.int32)[None, :]
    )
    fresh_scores = jnp.where(causal[None, :, None, None, :], fresh_scores, -1e30)
    top_score = jnp.maximum(jnp.max(cache_scores, axis=-1), jnp.max(fresh_scores, axis=-1))[
        ..., None
    ]
    cache_weights = jnp.exp(cache_scores - top_score)
    fresh_weights = jnp.exp(fresh_scores - top_score)
    total_weight = jnp.sum(cache_weights, axis=-1, keepdims=True) + jnp.sum(
        fresh_weights, axis=-1, keepdims=True
    )
    cache_probs = (cache_weights / total_weight).astype(jnp.bfloat16)
    fresh_probs = (fresh_weights / total_weight).astype(jnp.bfloat16)
    cache_vals = cached_value_rows.reshape(row_total, context, kv_local, head_size)
    fresh_vals = new_values.reshape(row_total, token_total, kv_local, head_size)
    mixed_out = jnp.einsum(
        "rthgj,rjhd->rthgd", cache_probs, cache_vals, preferred_element_type=jnp.float32
    )
    mixed_out = mixed_out + jnp.einsum(
        "rthgs,rshd->rthgd", fresh_probs, fresh_vals, preferred_element_type=jnp.float32
    )
    return mixed_out.reshape(row_total, token_total, query_width).astype(jnp.bfloat16)


def body(
    hidden,
    input_norm_gain,
    key_value_weight,
    adapter_down_weight,
    adapter_up_weight,
    request_adapter,
    queries,
    cached_key_rows,
    cached_value_rows,
    cached_length,
):
    row_count, token_count, model_width = hidden.shape
    feature_total = adapter_down_weight.shape[1]
    adapter_number = adapter_down_weight.shape[0]
    rank_total = adapter_down_weight.shape[2]
    rank_width = adapter_up_weight.shape[2]
    column_count = key_value_weight.shape[2]
    owner_count = lax.axis_size("adapter")
    cap = SLOT_CAPACITY
    slot_total = owner_count * cap

    values = hidden.astype(jnp.float32)
    meansq = jnp.mean(values * values, axis=-1, keepdims=True)
    row_scale = lax.rsqrt(meansq + epsilon)
    normed_input = (values * row_scale * input_norm_gain.astype(jnp.float32)).astype(jnp.bfloat16)
    base_proj = jnp.dot(
        normed_input.reshape(row_count * token_count, model_width),
        key_value_weight.reshape(model_width, 2 * column_count),
        preferred_element_type=jnp.float32,
    )
    base_proj = lax.optimization_barrier(base_proj.reshape(row_count, token_count, 2, column_count))

    owner_of = request_adapter // adapter_number
    local_adapter = request_adapter - owner_of * adapter_number
    row_ids = jnp.arange(row_count, dtype=jnp.int32)
    same_owner = owner_of[:, None] == owner_of[None, :]
    earlier = row_ids[None, :] < row_ids[:, None]
    rank_in_owner = jnp.sum((same_owner & earlier).astype(jnp.int32), axis=1)
    slot_of = owner_of * cap + rank_in_owner
    pick = (slot_of[None, :] == jnp.arange(slot_total, dtype=jnp.int32)[:, None]).astype(
        jnp.bfloat16
    )

    feature_start = lax.axis_index("tensor") * feature_total
    hidden_shard = lax.dynamic_slice_in_dim(hidden, feature_start, feature_total, 2)
    gain_shard = lax.dynamic_slice_in_dim(input_norm_gain, feature_start, feature_total, 0)
    own_features = (
        hidden_shard.astype(jnp.float32) * row_scale * gain_shard.astype(jnp.float32)
    ).astype(jnp.bfloat16)
    packed = jnp.dot(
        pick,
        own_features.reshape(row_count, token_count * feature_total),
        preferred_element_type=jnp.float32,
    ).astype(jnp.bfloat16)
    packed = packed.reshape(owner_count, cap * token_count, feature_total)
    slot_adapter = jnp.dot(
        pick, local_adapter.astype(jnp.bfloat16), preferred_element_type=jnp.float32
    ).astype(jnp.bfloat16)
    id_row = jnp.zeros((owner_count, 1, feature_total), jnp.bfloat16)
    id_row = lax.dynamic_update_slice(
        id_row, slot_adapter.reshape(owner_count, 1, cap), (0, 0, 0)
    )
    send = jnp.concatenate([packed, id_row], axis=1)
    recv = lax.all_to_all(send, "adapter", 0, 0, tiled=True)

    got_rows = recv[:, : cap * token_count].reshape(slot_total, token_count, feature_total)
    got_adapter = recv[:, cap * token_count, :cap].reshape(slot_total).astype(jnp.int32)
    selector = (
        got_adapter[:, None] == jnp.arange(adapter_number, dtype=jnp.int32)[None, :]
    ).astype(jnp.float32)

    down_all = jnp.einsum(
        "euz,nzs->euns", got_rows, adapter_down_weight, preferred_element_type=jnp.float32
    )
    partial_rank = jnp.sum(down_all * selector[:, None, :, None], axis=2)
    rank_hidden = lax.psum(partial_rank, "tensor").astype(jnp.bfloat16)

    rank_selector = selector.astype(jnp.bfloat16)
    masked = rank_hidden[:, :, None, :] * rank_selector[:, None, :, None]
    up_zero = jnp.zeros_like(adapter_up_weight[:, 0])
    up_blocks = jnp.stack(
        [
            jnp.concatenate([adapter_up_weight[:, 0], up_zero], axis=1),
            jnp.concatenate([up_zero, adapter_up_weight[:, 1]], axis=1),
        ],
        axis=2,
    )
    delta_slots = jnp.einsum(
        "gled,edkb->glkb", masked, up_blocks, preferred_element_type=jnp.float32
    )
    delta_send = delta_slots.reshape(owner_count, cap * token_count * 2, column_count)
    delta_recv = lax.all_to_all(delta_send, "adapter", 0, 0, tiled=True)
    delta_rows = delta_recv.reshape(slot_total, token_count * 2 * column_count)
    adapter_update = jnp.take(delta_rows, slot_of, axis=0).reshape(
        row_count, token_count, 2, column_count
    )

    projected_output = base_proj + adapter_update
    positions = (cached_length[:, None] + jnp.arange(token_count, dtype=jnp.int32)[None, :]).astype(
        jnp.float32
    )
    kv_local = column_count // HEAD_DIM
    key_vecs = rotate_keys(
        projected_output[:, :, 0].reshape(row_count, token_count, kv_local, HEAD_DIM),
        positions[:, :, None],
    )
    new_keys = key_vecs.reshape(row_count, token_count, column_count).astype(jnp.bfloat16)
    new_values = projected_output[:, :, 1].astype(jnp.bfloat16)
    attended = attend(
        queries, cached_key_rows, cached_value_rows, cached_length, new_keys, new_values, HEAD_DIM
    )
    return (new_keys, new_values, attended)


def solution(mesh):
    in_specs = (
        P("adapter", None, None),
        P(),
        P(None, None, "tensor"),
        P("adapter", "tensor", None),
        P("adapter", None, None, "tensor"),
        P("adapter"),
        P("adapter", None, "tensor"),
        P("adapter", None, "tensor"),
        P("adapter", None, "tensor"),
        P("adapter"),
    )
    out_specs = (
        P("adapter", None, "tensor"),
        P("adapter", None, "tensor"),
        P("adapter", None, "tensor"),
    )
    return jax.shard_map(body, mesh=mesh, in_specs=in_specs, out_specs=out_specs, check_vma=False)
```

```python
import jax
import jax.numpy as jnp
from jax import lax
from jax.sharding import Mesh, PartitionSpec as P

HEAD_DIM = 128
SLOT_CAPACITY = 6


epsilon = 1e-05
rope_base = 500000.0


def rotate_keys(key_vecs, positions):
    head_size = key_vecs.shape[-1]
    half_size = head_size // 2
    inverse = rope_base ** (-(jnp.arange(half_size, dtype=jnp.float32) * 2.0 / head_size))
    angles = positions[..., None] * inverse
    cosine = jnp.cos(angles)
    sine_part = jnp.sin(angles)
    first_half = key_vecs[..., :half_size]
    second = key_vecs[..., half_size:]
    return jnp.concatenate(
        [first_half * cosine - second * sine_part, second * cosine + first_half * sine_part],
        axis=-1,
    )


def normalize(hidden, input_norm_gain):
    values = hidden.astype(jnp.float32)
    meansq = jnp.mean(values * values, axis=-1, keepdims=True)
    return (values * lax.rsqrt(meansq + epsilon) * input_norm_gain.astype(jnp.float32)).astype(
        jnp.bfloat16
    )


def attend(
    queries, cached_key_rows, cached_value_rows, cached_length, new_keys, new_values, head_size
):
    row_total, token_total, query_width = queries.shape
    context = cached_key_rows.shape[1]
    kv_local = cached_key_rows.shape[2] // head_size
    group_size = query_width // (kv_local * head_size)
    score_scale = float(head_size) ** (-0.5)
    query_vecs = queries.reshape(row_total, token_total, kv_local, group_size, head_size)
    cache_vecs = cached_key_rows.reshape(row_total, context, kv_local, head_size)
    fresh_vecs = new_keys.reshape(row_total, token_total, kv_local, head_size)
    cache_scores = (
        jnp.einsum("rthgd,rjhd->rthgj", query_vecs, cache_vecs, preferred_element_type=jnp.float32)
        * score_scale
    )
    slot_live = jnp.arange(context, dtype=jnp.int32)[None, :] < cached_length[:, None]
    cache_scores = jnp.where(slot_live[:, None, None, None, :], cache_scores, -1e30)
    fresh_scores = (
        jnp.einsum("rthgd,rshd->rthgs", query_vecs, fresh_vecs, preferred_element_type=jnp.float32)
        * score_scale
    )
    causal = (
        jnp.arange(token_total, dtype=jnp.int32)[:, None]
        >= jnp.arange(token_total, dtype=jnp.int32)[None, :]
    )
    fresh_scores = jnp.where(causal[None, :, None, None, :], fresh_scores, -1e30)
    top_score = jnp.maximum(jnp.max(cache_scores, axis=-1), jnp.max(fresh_scores, axis=-1))[
        ..., None
    ]
    cache_weights = jnp.exp(cache_scores - top_score)
    fresh_weights = jnp.exp(fresh_scores - top_score)
    total_weight = jnp.sum(cache_weights, axis=-1, keepdims=True) + jnp.sum(
        fresh_weights, axis=-1, keepdims=True
    )
    cache_probs = (cache_weights / total_weight).astype(jnp.bfloat16)
    fresh_probs = (fresh_weights / total_weight).astype(jnp.bfloat16)
    cache_vals = cached_value_rows.reshape(row_total, context, kv_local, head_size)
    fresh_vals = new_values.reshape(row_total, token_total, kv_local, head_size)
    mixed_out = jnp.einsum(
        "rthgj,rjhd->rthgd", cache_probs, cache_vals, preferred_element_type=jnp.float32
    )
    mixed_out = mixed_out + jnp.einsum(
        "rthgs,rshd->rthgd", fresh_probs, fresh_vals, preferred_element_type=jnp.float32
    )
    return mixed_out.reshape(row_total, token_total, query_width).astype(jnp.bfloat16)


def exchange(blocks):
    z_count = lax.axis_size("az")
    y_count = lax.axis_size("ay")
    grid = blocks.reshape((z_count, y_count) + blocks.shape[1:])
    grid = lax.all_to_all(grid, "ay", 1, 1, tiled=True)
    grid = lax.all_to_all(grid, "az", 0, 0, tiled=True)
    return grid.reshape(blocks.shape)


def body(
    hidden,
    input_norm_gain,
    key_value_weight,
    adapter_down_weight,
    adapter_up_weight,
    request_adapter,
    queries,
    cached_key_rows,
    cached_value_rows,
    cached_length,
):
    row_count, token_count, model_width = hidden.shape
    feature_total = adapter_down_weight.shape[1]
    adapter_number = adapter_down_weight.shape[0]
    rank_total = adapter_down_weight.shape[2]
    rank_width = adapter_up_weight.shape[2]
    column_count = key_value_weight.shape[2]
    owner_count = lax.axis_size("az") * lax.axis_size("ay")
    cap = SLOT_CAPACITY
    slot_total = owner_count * cap

    values = hidden.astype(jnp.float32)
    meansq = jnp.mean(values * values, axis=-1, keepdims=True)
    row_scale = lax.rsqrt(meansq + epsilon)
    normed_input = (values * row_scale * input_norm_gain.astype(jnp.float32)).astype(jnp.bfloat16)
    base_proj = jnp.dot(
        normed_input.reshape(row_count * token_count, model_width),
        key_value_weight.reshape(model_width, 2 * column_count),
        preferred_element_type=jnp.float32,
    )
    base_proj = lax.optimization_barrier(base_proj.reshape(row_count, token_count, 2, column_count))

    owner_of = request_adapter // adapter_number
    local_adapter = request_adapter - owner_of * adapter_number
    row_ids = jnp.arange(row_count, dtype=jnp.int32)
    same_owner = owner_of[:, None] == owner_of[None, :]
    earlier = row_ids[None, :] < row_ids[:, None]
    rank_in_owner = jnp.sum((same_owner & earlier).astype(jnp.int32), axis=1)
    slot_of = owner_of * cap + rank_in_owner
    pick = (slot_of[None, :] == jnp.arange(slot_total, dtype=jnp.int32)[:, None]).astype(
        jnp.bfloat16
    )

    feature_start = (lax.axis_index("tx") * lax.axis_size("tc") + lax.axis_index("tc")) * feature_total
    hidden_shard = lax.dynamic_slice_in_dim(hidden, feature_start, feature_total, 2)
    gain_shard = lax.dynamic_slice_in_dim(input_norm_gain, feature_start, feature_total, 0)
    own_features = (
        hidden_shard.astype(jnp.float32) * row_scale * gain_shard.astype(jnp.float32)
    ).astype(jnp.bfloat16)
    packed = jnp.dot(
        pick,
        own_features.reshape(row_count, token_count * feature_total),
        preferred_element_type=jnp.float32,
    ).astype(jnp.bfloat16)
    packed = packed.reshape(owner_count, cap * token_count, feature_total)
    slot_adapter = jnp.dot(
        pick, local_adapter.astype(jnp.bfloat16), preferred_element_type=jnp.float32
    ).astype(jnp.bfloat16)
    id_row = jnp.zeros((owner_count, 1, feature_total), jnp.bfloat16)
    id_row = lax.dynamic_update_slice(
        id_row, slot_adapter.reshape(owner_count, 1, cap), (0, 0, 0)
    )
    send = jnp.concatenate([packed, id_row], axis=1)
    recv = exchange(send)

    got_rows = recv[:, : cap * token_count].reshape(slot_total, token_count, feature_total)
    got_adapter = recv[:, cap * token_count, :cap].reshape(slot_total).astype(jnp.int32)
    selector = (
        got_adapter[:, None] == jnp.arange(adapter_number, dtype=jnp.int32)[None, :]
    ).astype(jnp.float32)

    down_all = jnp.einsum(
        "euz,nzs->euns", got_rows, adapter_down_weight, preferred_element_type=jnp.float32
    )
    partial_rank = jnp.sum(down_all * selector[:, None, :, None], axis=2)
    rank_hidden = lax.psum(partial_rank, ("tx", "tc")).astype(jnp.bfloat16)

    rank_selector = selector.astype(jnp.bfloat16)
    masked = rank_hidden[:, :, None, :] * rank_selector[:, None, :, None]
    key_part = jnp.einsum(
        "gled,edb->glb",
        masked[..., :rank_width],
        adapter_up_weight[:, 0],
        preferred_element_type=jnp.float32,
    )
    value_part = jnp.einsum(
        "gled,edb->glb",
        masked[..., rank_width:],
        adapter_up_weight[:, 1],
        preferred_element_type=jnp.float32,
    )
    delta_slots = jnp.stack([key_part, value_part], axis=2)
    delta_send = delta_slots.reshape(owner_count, cap * token_count * 2, column_count)
    delta_recv = exchange(delta_send)
    delta_rows = delta_recv.reshape(slot_total, token_count * 2 * column_count)
    adapter_update = jnp.take(delta_rows, slot_of, axis=0).reshape(
        row_count, token_count, 2, column_count
    )

    projected_output = base_proj + adapter_update
    positions = (cached_length[:, None] + jnp.arange(token_count, dtype=jnp.int32)[None, :]).astype(
        jnp.float32
    )
    kv_local = column_count // HEAD_DIM
    key_vecs = rotate_keys(
        projected_output[:, :, 0].reshape(row_count, token_count, kv_local, HEAD_DIM),
        positions[:, :, None],
    )
    new_keys = key_vecs.reshape(row_count, token_count, column_count).astype(jnp.bfloat16)
    new_values = projected_output[:, :, 1].astype(jnp.bfloat16)
    attended = attend(
        queries, cached_key_rows, cached_value_rows, cached_length, new_keys, new_values, HEAD_DIM
    )
    return (new_keys, new_values, attended)


def solution(mesh):
    owner_devices = mesh.devices.shape[0]
    tensor_devices = mesh.devices.shape[1]
    y_count = 4 if owner_devices % 4 == 0 else 1
    core_count = 2 if tensor_devices % 2 == 0 else 1
    split_mesh = Mesh(
        mesh.devices.reshape(
            owner_devices // y_count, y_count, tensor_devices // core_count, core_count
        ),
        ("az", "ay", "tx", "tc"),
    )
    adapter = ("az", "ay")
    tensor = ("tx", "tc")
    in_specs = (
        P(adapter, None, None),
        P(),
        P(None, None, tensor),
        P(adapter, tensor, None),
        P(adapter, None, None, tensor),
        P(adapter),
        P(adapter, None, tensor),
        P(adapter, None, tensor),
        P(adapter, None, tensor),
        P(adapter),
    )
    out_specs = (
        P(adapter, None, tensor),
        P(adapter, None, tensor),
        P(adapter, None, tensor),
    )
    return jax.shard_map(
        body, mesh=split_mesh, in_specs=in_specs, out_specs=out_specs, check_vma=False
    )
```

```python
import jax
import jax.numpy as jnp
from jax import lax
from jax.sharding import PartitionSpec as P

HEAD_DIM = 128
SLOT_CAPACITY = 6


epsilon = 1e-05
rope_base = 500000.0


def rotate_keys(key_vecs, positions):
    head_size = key_vecs.shape[-1]
    half_size = head_size // 2
    inverse = rope_base ** (-(jnp.arange(half_size, dtype=jnp.float32) * 2.0 / head_size))
    angles = positions[..., None] * inverse
    cosine = jnp.cos(angles)
    sine_part = jnp.sin(angles)
    first_half = key_vecs[..., :half_size]
    second = key_vecs[..., half_size:]
    return jnp.concatenate(
        [first_half * cosine - second * sine_part, second * cosine + first_half * sine_part],
        axis=-1,
    )


def normalize(hidden, input_norm_gain):
    values = hidden.astype(jnp.float32)
    meansq = jnp.mean(values * values, axis=-1, keepdims=True)
    return (values * lax.rsqrt(meansq + epsilon) * input_norm_gain.astype(jnp.float32)).astype(
        jnp.bfloat16
    )


def attend(
    queries, cached_key_rows, cached_value_rows, cached_length, new_keys, new_values, head_size
):
    row_total, token_total, query_width = queries.shape
    context = cached_key_rows.shape[1]
    kv_local = cached_key_rows.shape[2] // head_size
    group_size = query_width // (kv_local * head_size)
    score_scale = float(head_size) ** (-0.5)
    query_vecs = queries.reshape(row_total, token_total, kv_local, group_size, head_size)
    cache_vecs = cached_key_rows.reshape(row_total, context, kv_local, head_size)
    fresh_vecs = new_keys.reshape(row_total, token_total, kv_local, head_size)
    cache_scores = (
        jnp.einsum("rthgd,rjhd->rthgj", query_vecs, cache_vecs, preferred_element_type=jnp.float32)
        * score_scale
    )
    slot_live = jnp.arange(context, dtype=jnp.int32)[None, :] < cached_length[:, None]
    cache_scores = jnp.where(slot_live[:, None, None, None, :], cache_scores, -1e30)
    fresh_scores = (
        jnp.einsum("rthgd,rshd->rthgs", query_vecs, fresh_vecs, preferred_element_type=jnp.float32)
        * score_scale
    )
    causal = (
        jnp.arange(token_total, dtype=jnp.int32)[:, None]
        >= jnp.arange(token_total, dtype=jnp.int32)[None, :]
    )
    fresh_scores = jnp.where(causal[None, :, None, None, :], fresh_scores, -1e30)
    top_score = jnp.maximum(jnp.max(cache_scores, axis=-1), jnp.max(fresh_scores, axis=-1))[
        ..., None
    ]
    cache_weights = jnp.exp(cache_scores - top_score)
    fresh_weights = jnp.exp(fresh_scores - top_score)
    total_weight = jnp.sum(cache_weights, axis=-1, keepdims=True) + jnp.sum(
        fresh_weights, axis=-1, keepdims=True
    )
    cache_probs = (cache_weights / total_weight).astype(jnp.bfloat16)
    fresh_probs = (fresh_weights / total_weight).astype(jnp.bfloat16)
    cache_vals = cached_value_rows.reshape(row_total, context, kv_local, head_size)
    fresh_vals = new_values.reshape(row_total, token_total, kv_local, head_size)
    mixed_out = jnp.einsum(
        "rthgj,rjhd->rthgd", cache_probs, cache_vals, preferred_element_type=jnp.float32
    )
    mixed_out = mixed_out + jnp.einsum(
        "rthgs,rshd->rthgd", fresh_probs, fresh_vals, preferred_element_type=jnp.float32
    )
    return mixed_out.reshape(row_total, token_total, query_width).astype(jnp.bfloat16)


def butterfly_sum(value, axis_name):
    member_count = lax.axis_size(axis_name)
    stride = 1
    while stride < member_count:
        pairs = [(i, i ^ stride) for i in range(member_count)]
        value = value + lax.ppermute(value, axis_name, pairs)
        stride *= 2
    return value


def body(
    hidden,
    input_norm_gain,
    key_value_weight,
    adapter_down_weight,
    adapter_up_weight,
    request_adapter,
    queries,
    cached_key_rows,
    cached_value_rows,
    cached_length,
):
    row_count, token_count, model_width = hidden.shape
    feature_total = adapter_down_weight.shape[1]
    adapter_number = adapter_down_weight.shape[0]
    rank_total = adapter_down_weight.shape[2]
    rank_width = adapter_up_weight.shape[2]
    column_count = key_value_weight.shape[2]
    owner_count = lax.axis_size("adapter")
    cap = SLOT_CAPACITY
    slot_total = owner_count * cap

    values = hidden.astype(jnp.float32)
    meansq = jnp.mean(values * values, axis=-1, keepdims=True)
    row_scale = lax.rsqrt(meansq + epsilon)
    normed_input = (values * row_scale * input_norm_gain.astype(jnp.float32)).astype(jnp.bfloat16)
    base_proj = jnp.dot(
        normed_input.reshape(row_count * token_count, model_width),
        key_value_weight.reshape(model_width, 2 * column_count),
        preferred_element_type=jnp.float32,
    )
    base_proj = lax.optimization_barrier(base_proj.reshape(row_count, token_count, 2, column_count))

    owner_of = request_adapter // adapter_number
    local_adapter = request_adapter - owner_of * adapter_number
    row_ids = jnp.arange(row_count, dtype=jnp.int32)
    same_owner = owner_of[:, None] == owner_of[None, :]
    earlier = row_ids[None, :] < row_ids[:, None]
    rank_in_owner = jnp.sum((same_owner & earlier).astype(jnp.int32), axis=1)
    slot_of = owner_of * cap + rank_in_owner
    pick = (slot_of[None, :] == jnp.arange(slot_total, dtype=jnp.int32)[:, None]).astype(
        jnp.bfloat16
    )

    feature_start = lax.axis_index("tensor") * feature_total
    hidden_shard = lax.dynamic_slice_in_dim(hidden, feature_start, feature_total, 2)
    gain_shard = lax.dynamic_slice_in_dim(input_norm_gain, feature_start, feature_total, 0)
    own_features = (
        hidden_shard.astype(jnp.float32) * row_scale * gain_shard.astype(jnp.float32)
    ).astype(jnp.bfloat16)
    packed = jnp.dot(
        pick,
        own_features.reshape(row_count, token_count * feature_total),
        preferred_element_type=jnp.float32,
    ).astype(jnp.bfloat16)
    packed = packed.reshape(owner_count, cap * token_count, feature_total)
    slot_adapter = jnp.dot(
        pick, local_adapter.astype(jnp.bfloat16), preferred_element_type=jnp.float32
    ).astype(jnp.bfloat16)
    id_row = jnp.zeros((owner_count, 1, feature_total), jnp.bfloat16)
    id_row = lax.dynamic_update_slice(
        id_row, slot_adapter.reshape(owner_count, 1, cap), (0, 0, 0)
    )
    send = jnp.concatenate([packed, id_row], axis=1)
    recv = lax.all_to_all(send, "adapter", 0, 0, tiled=True)

    got_rows = recv[:, : cap * token_count].reshape(slot_total, token_count, feature_total)
    got_adapter = recv[:, cap * token_count, :cap].reshape(slot_total).astype(jnp.int32)
    selector = (
        got_adapter[:, None] == jnp.arange(adapter_number, dtype=jnp.int32)[None, :]
    ).astype(jnp.float32)

    down_all = jnp.einsum(
        "euz,nzs->euns", got_rows, adapter_down_weight, preferred_element_type=jnp.float32
    )
    partial_rank = jnp.sum(down_all * selector[:, None, :, None], axis=2)
    rank_hidden = butterfly_sum(partial_rank, "tensor").astype(jnp.bfloat16)

    rank_selector = selector.astype(jnp.bfloat16)
    masked = rank_hidden[:, :, None, :] * rank_selector[:, None, :, None]
    key_part = jnp.einsum(
        "gled,edb->glb",
        masked[..., :rank_width],
        adapter_up_weight[:, 0],
        preferred_element_type=jnp.float32,
    )
    value_part = jnp.einsum(
        "gled,edb->glb",
        masked[..., rank_width:],
        adapter_up_weight[:, 1],
        preferred_element_type=jnp.float32,
    )
    delta_slots = jnp.stack([key_part, value_part], axis=2)
    delta_send = delta_slots.reshape(owner_count, cap * token_count * 2, column_count)
    delta_recv = lax.all_to_all(delta_send, "adapter", 0, 0, tiled=True)
    delta_rows = delta_recv.reshape(slot_total, token_count * 2 * column_count)
    adapter_update = jnp.take(delta_rows, slot_of, axis=0).reshape(
        row_count, token_count, 2, column_count
    )

    projected_output = base_proj + adapter_update
    positions = (cached_length[:, None] + jnp.arange(token_count, dtype=jnp.int32)[None, :]).astype(
        jnp.float32
    )
    kv_local = column_count // HEAD_DIM
    key_vecs = rotate_keys(
        projected_output[:, :, 0].reshape(row_count, token_count, kv_local, HEAD_DIM),
        positions[:, :, None],
    )
    new_keys = key_vecs.reshape(row_count, token_count, column_count).astype(jnp.bfloat16)
    new_values = projected_output[:, :, 1].astype(jnp.bfloat16)
    attended = attend(
        queries, cached_key_rows, cached_value_rows, cached_length, new_keys, new_values, HEAD_DIM
    )
    return (new_keys, new_values, attended)


def solution(mesh):
    in_specs = (
        P("adapter", None, None),
        P(),
        P(None, None, "tensor"),
        P("adapter", "tensor", None),
        P("adapter", None, None, "tensor"),
        P("adapter"),
        P("adapter", None, "tensor"),
        P("adapter", None, "tensor"),
        P("adapter", None, "tensor"),
        P("adapter"),
    )
    out_specs = (
        P("adapter", None, "tensor"),
        P("adapter", None, "tensor"),
        P("adapter", None, "tensor"),
    )
    return jax.shard_map(body, mesh=mesh, in_specs=in_specs, out_specs=out_specs, check_vma=False)
```

```python
import jax
import jax.numpy as jnp
from jax import lax
from jax.sharding import PartitionSpec as P

HEAD_DIM = 128
SLOT_CAPACITY = 6


epsilon = 1e-05
rope_base = 500000.0


def rotate_keys(key_vecs, positions):
    head_size = key_vecs.shape[-1]
    half_size = head_size // 2
    inverse = rope_base ** (-(jnp.arange(half_size, dtype=jnp.float32) * 2.0 / head_size))
    angles = positions[..., None] * inverse
    cosine = jnp.cos(angles)
    sine_part = jnp.sin(angles)
    first_half = key_vecs[..., :half_size]
    second = key_vecs[..., half_size:]
    return jnp.concatenate(
        [first_half * cosine - second * sine_part, second * cosine + first_half * sine_part],
        axis=-1,
    )


def normalize(hidden, input_norm_gain):
    values = hidden.astype(jnp.float32)
    meansq = jnp.mean(values * values, axis=-1, keepdims=True)
    return (values * lax.rsqrt(meansq + epsilon) * input_norm_gain.astype(jnp.float32)).astype(
        jnp.bfloat16
    )


def attend(
    queries, cached_key_rows, cached_value_rows, cached_length, new_keys, new_values, head_size
):
    row_total, token_total, query_width = queries.shape
    context = cached_key_rows.shape[1]
    kv_local = cached_key_rows.shape[2] // head_size
    group_size = query_width // (kv_local * head_size)
    score_scale = float(head_size) ** (-0.5)
    query_vecs = queries.reshape(row_total, token_total, kv_local, group_size, head_size)
    cache_vecs = cached_key_rows.reshape(row_total, context, kv_local, head_size)
    fresh_vecs = new_keys.reshape(row_total, token_total, kv_local, head_size)
    cache_scores = (
        jnp.einsum("rthgd,rjhd->rthgj", query_vecs, cache_vecs, preferred_element_type=jnp.float32)
        * score_scale
    )
    slot_live = jnp.arange(context, dtype=jnp.int32)[None, :] < cached_length[:, None]
    cache_scores = jnp.where(slot_live[:, None, None, None, :], cache_scores, -1e30)
    fresh_scores = (
        jnp.einsum("rthgd,rshd->rthgs", query_vecs, fresh_vecs, preferred_element_type=jnp.float32)
        * score_scale
    )
    causal = (
        jnp.arange(token_total, dtype=jnp.int32)[:, None]
        >= jnp.arange(token_total, dtype=jnp.int32)[None, :]
    )
    fresh_scores = jnp.where(causal[None, :, None, None, :], fresh_scores, -1e30)
    top_score = jnp.maximum(jnp.max(cache_scores, axis=-1), jnp.max(fresh_scores, axis=-1))[
        ..., None
    ]
    cache_weights = jnp.exp(cache_scores - top_score)
    fresh_weights = jnp.exp(fresh_scores - top_score)
    total_weight = jnp.sum(cache_weights, axis=-1, keepdims=True) + jnp.sum(
        fresh_weights, axis=-1, keepdims=True
    )
    cache_probs = (cache_weights / total_weight).astype(jnp.bfloat16)
    fresh_probs = (fresh_weights / total_weight).astype(jnp.bfloat16)
    cache_vals = cached_value_rows.reshape(row_total, context, kv_local, head_size)
    fresh_vals = new_values.reshape(row_total, token_total, kv_local, head_size)
    mixed_out = jnp.einsum(
        "rthgj,rjhd->rthgd", cache_probs, cache_vals, preferred_element_type=jnp.float32
    )
    mixed_out = mixed_out + jnp.einsum(
        "rthgs,rshd->rthgd", fresh_probs, fresh_vals, preferred_element_type=jnp.float32
    )
    return mixed_out.reshape(row_total, token_total, query_width).astype(jnp.bfloat16)


def butterfly_sum(value, axis_name):
    member_count = lax.axis_size(axis_name)
    value = value + lax.ppermute(value, axis_name, [(i, i ^ 1) for i in range(member_count)])
    shifted = [
        lax.ppermute(value, axis_name, [(i, (i + 2 * k) % member_count) for i in range(member_count)])
        for k in (1, 2, 3)
    ]
    return (value + shifted[1]) + (shifted[0] + shifted[2])


def body(
    hidden,
    input_norm_gain,
    key_value_weight,
    adapter_down_weight,
    adapter_up_weight,
    request_adapter,
    queries,
    cached_key_rows,
    cached_value_rows,
    cached_length,
):
    row_count, token_count, model_width = hidden.shape
    feature_total = adapter_down_weight.shape[1]
    adapter_number = adapter_down_weight.shape[0]
    rank_total = adapter_down_weight.shape[2]
    rank_width = adapter_up_weight.shape[2]
    column_count = key_value_weight.shape[2]
    owner_count = lax.axis_size("adapter")
    cap = SLOT_CAPACITY
    slot_total = owner_count * cap

    values = hidden.astype(jnp.float32)
    meansq = jnp.mean(values * values, axis=-1, keepdims=True)
    row_scale = lax.rsqrt(meansq + epsilon)
    normed_input = (values * row_scale * input_norm_gain.astype(jnp.float32)).astype(jnp.bfloat16)
    base_proj = jnp.dot(
        normed_input.reshape(row_count * token_count, model_width),
        key_value_weight.reshape(model_width, 2 * column_count),
        preferred_element_type=jnp.float32,
    )
    base_proj = lax.optimization_barrier(base_proj.reshape(row_count, token_count, 2, column_count))

    owner_of = request_adapter // adapter_number
    local_adapter = request_adapter - owner_of * adapter_number
    row_ids = jnp.arange(row_count, dtype=jnp.int32)
    same_owner = owner_of[:, None] == owner_of[None, :]
    earlier = row_ids[None, :] < row_ids[:, None]
    rank_in_owner = jnp.sum((same_owner & earlier).astype(jnp.int32), axis=1)
    slot_of = owner_of * cap + rank_in_owner
    pick = (slot_of[None, :] == jnp.arange(slot_total, dtype=jnp.int32)[:, None]).astype(
        jnp.bfloat16
    )

    feature_start = lax.axis_index("tensor") * feature_total
    hidden_shard = lax.dynamic_slice_in_dim(hidden, feature_start, feature_total, 2)
    gain_shard = lax.dynamic_slice_in_dim(input_norm_gain, feature_start, feature_total, 0)
    own_features = (
        hidden_shard.astype(jnp.float32) * row_scale * gain_shard.astype(jnp.float32)
    ).astype(jnp.bfloat16)
    packed = jnp.dot(
        pick,
        own_features.reshape(row_count, token_count * feature_total),
        preferred_element_type=jnp.float32,
    ).astype(jnp.bfloat16)
    packed = packed.reshape(owner_count, cap * token_count, feature_total)
    slot_adapter = jnp.dot(
        pick, local_adapter.astype(jnp.bfloat16), preferred_element_type=jnp.float32
    ).astype(jnp.bfloat16)
    id_row = jnp.zeros((owner_count, 1, feature_total), jnp.bfloat16)
    id_row = lax.dynamic_update_slice(
        id_row, slot_adapter.reshape(owner_count, 1, cap), (0, 0, 0)
    )
    send = jnp.concatenate([packed, id_row], axis=1)
    recv = lax.all_to_all(send, "adapter", 0, 0, tiled=True)

    got_rows = recv[:, : cap * token_count].reshape(slot_total, token_count, feature_total)
    got_adapter = recv[:, cap * token_count, :cap].reshape(slot_total).astype(jnp.int32)
    selector = (
        got_adapter[:, None] == jnp.arange(adapter_number, dtype=jnp.int32)[None, :]
    ).astype(jnp.float32)

    down_all = jnp.einsum(
        "euz,nzs->euns", got_rows, adapter_down_weight, preferred_element_type=jnp.float32
    )
    partial_rank = jnp.sum(down_all * selector[:, None, :, None], axis=2)
    rank_hidden = butterfly_sum(partial_rank, "tensor").astype(jnp.bfloat16)

    rank_selector = selector.astype(jnp.bfloat16)
    masked = rank_hidden[:, :, None, :] * rank_selector[:, None, :, None]
    key_part = jnp.einsum(
        "gled,edb->glb",
        masked[..., :rank_width],
        adapter_up_weight[:, 0],
        preferred_element_type=jnp.float32,
    )
    value_part = jnp.einsum(
        "gled,edb->glb",
        masked[..., rank_width:],
        adapter_up_weight[:, 1],
        preferred_element_type=jnp.float32,
    )
    delta_slots = jnp.stack([key_part, value_part], axis=2)
    delta_send = delta_slots.reshape(owner_count, cap * token_count * 2, column_count)
    delta_recv = lax.all_to_all(delta_send, "adapter", 0, 0, tiled=True)
    delta_rows = delta_recv.reshape(slot_total, token_count * 2 * column_count)
    adapter_update = jnp.take(delta_rows, slot_of, axis=0).reshape(
        row_count, token_count, 2, column_count
    )

    projected_output = base_proj + adapter_update
    positions = (cached_length[:, None] + jnp.arange(token_count, dtype=jnp.int32)[None, :]).astype(
        jnp.float32
    )
    kv_local = column_count // HEAD_DIM
    key_vecs = rotate_keys(
        projected_output[:, :, 0].reshape(row_count, token_count, kv_local, HEAD_DIM),
        positions[:, :, None],
    )
    new_keys = key_vecs.reshape(row_count, token_count, column_count).astype(jnp.bfloat16)
    new_values = projected_output[:, :, 1].astype(jnp.bfloat16)
    attended = attend(
        queries, cached_key_rows, cached_value_rows, cached_length, new_keys, new_values, HEAD_DIM
    )
    return (new_keys, new_values, attended)


def solution(mesh):
    in_specs = (
        P("adapter", None, None),
        P(),
        P(None, None, "tensor"),
        P("adapter", "tensor", None),
        P("adapter", None, None, "tensor"),
        P("adapter"),
        P("adapter", None, "tensor"),
        P("adapter", None, "tensor"),
        P("adapter", None, "tensor"),
        P("adapter"),
    )
    out_specs = (
        P("adapter", None, "tensor"),
        P("adapter", None, "tensor"),
        P("adapter", None, "tensor"),
    )
    return jax.shard_map(body, mesh=mesh, in_specs=in_specs, out_specs=out_specs, check_vma=False)
```

```python
import jax
import jax.numpy as jnp
from jax import lax
from jax.sharding import PartitionSpec as P

HEAD_DIM = 128
SLOT_CAPACITY = 6


epsilon = 1e-05
rope_base = 500000.0


def rotate_keys(key_vecs, positions):
    head_size = key_vecs.shape[-1]
    half_size = head_size // 2
    inverse = rope_base ** (-(jnp.arange(half_size, dtype=jnp.float32) * 2.0 / head_size))
    angles = positions[..., None] * inverse
    cosine = jnp.cos(angles)
    sine_part = jnp.sin(angles)
    first_half = key_vecs[..., :half_size]
    second = key_vecs[..., half_size:]
    return jnp.concatenate(
        [first_half * cosine - second * sine_part, second * cosine + first_half * sine_part],
        axis=-1,
    )


def normalize(hidden, input_norm_gain):
    values = hidden.astype(jnp.float32)
    meansq = jnp.mean(values * values, axis=-1, keepdims=True)
    return (values * lax.rsqrt(meansq + epsilon) * input_norm_gain.astype(jnp.float32)).astype(
        jnp.bfloat16
    )


def attend(
    queries, cached_key_rows, cached_value_rows, cached_length, new_keys, new_values, head_size
):
    row_total, token_total, query_width = queries.shape
    context = cached_key_rows.shape[1]
    kv_local = cached_key_rows.shape[2] // head_size
    group_size = query_width // (kv_local * head_size)
    score_scale = float(head_size) ** (-0.5)
    query_vecs = queries.reshape(row_total, token_total, kv_local, group_size, head_size)
    cache_vecs = cached_key_rows.reshape(row_total, context, kv_local, head_size)
    fresh_vecs = new_keys.reshape(row_total, token_total, kv_local, head_size)
    cache_scores = (
        jnp.einsum("rthgd,rjhd->rthgj", query_vecs, cache_vecs, preferred_element_type=jnp.float32)
        * score_scale
    )
    slot_live = jnp.arange(context, dtype=jnp.int32)[None, :] < cached_length[:, None]
    cache_scores = jnp.where(slot_live[:, None, None, None, :], cache_scores, -1e30)
    fresh_scores = (
        jnp.einsum("rthgd,rshd->rthgs", query_vecs, fresh_vecs, preferred_element_type=jnp.float32)
        * score_scale
    )
    causal = (
        jnp.arange(token_total, dtype=jnp.int32)[:, None]
        >= jnp.arange(token_total, dtype=jnp.int32)[None, :]
    )
    fresh_scores = jnp.where(causal[None, :, None, None, :], fresh_scores, -1e30)
    top_score = jnp.maximum(jnp.max(cache_scores, axis=-1), jnp.max(fresh_scores, axis=-1))[
        ..., None
    ]
    cache_weights = jnp.exp(cache_scores - top_score)
    fresh_weights = jnp.exp(fresh_scores - top_score)
    total_weight = jnp.sum(cache_weights, axis=-1, keepdims=True) + jnp.sum(
        fresh_weights, axis=-1, keepdims=True
    )
    cache_probs = (cache_weights / total_weight).astype(jnp.bfloat16)
    fresh_probs = (fresh_weights / total_weight).astype(jnp.bfloat16)
    cache_vals = cached_value_rows.reshape(row_total, context, kv_local, head_size)
    fresh_vals = new_values.reshape(row_total, token_total, kv_local, head_size)
    mixed_out = jnp.einsum(
        "rthgj,rjhd->rthgd", cache_probs, cache_vals, preferred_element_type=jnp.float32
    )
    mixed_out = mixed_out + jnp.einsum(
        "rthgs,rshd->rthgd", fresh_probs, fresh_vals, preferred_element_type=jnp.float32
    )
    return mixed_out.reshape(row_total, token_total, query_width).astype(jnp.bfloat16)


def butterfly_sum(value, axis_name):
    member_count = lax.axis_size(axis_name)
    value = value + lax.ppermute(value, axis_name, [(i, i ^ 1) for i in range(member_count)])
    shifted = [
        lax.ppermute(value, axis_name, [(i, (i + 2 * k) % member_count) for i in range(member_count)])
        for k in (1, 2, 3)
    ]
    return (value + shifted[1]) + (shifted[0] + shifted[2])


def body(
    hidden,
    input_norm_gain,
    key_value_weight,
    adapter_down_weight,
    adapter_up_weight,
    request_adapter,
    queries,
    cached_key_rows,
    cached_value_rows,
    cached_length,
):
    row_count, token_count, model_width = hidden.shape
    feature_total = adapter_down_weight.shape[1]
    adapter_number = adapter_down_weight.shape[0]
    rank_total = adapter_down_weight.shape[2]
    rank_width = adapter_up_weight.shape[2]
    column_count = key_value_weight.shape[2]
    owner_count = lax.axis_size("adapter")
    cap = SLOT_CAPACITY
    slot_total = owner_count * cap

    values = hidden.astype(jnp.float32)
    meansq = jnp.mean(values * values, axis=-1, keepdims=True)
    row_scale = lax.rsqrt(meansq + epsilon)
    normed_input = (values * row_scale * input_norm_gain.astype(jnp.float32)).astype(jnp.bfloat16)
    base_proj = jnp.dot(
        normed_input.reshape(row_count * token_count, model_width),
        key_value_weight.reshape(model_width, 2 * column_count),
        preferred_element_type=jnp.float32,
    )
    base_proj = lax.optimization_barrier(base_proj.reshape(row_count, token_count, 2, column_count))

    owner_of = request_adapter // adapter_number
    local_adapter = request_adapter - owner_of * adapter_number
    row_ids = jnp.arange(row_count, dtype=jnp.int32)
    same_owner = owner_of[:, None] == owner_of[None, :]
    earlier = row_ids[None, :] < row_ids[:, None]
    rank_in_owner = jnp.sum((same_owner & earlier).astype(jnp.int32), axis=1)
    slot_of = owner_of * cap + rank_in_owner
    pick = (slot_of[None, :] == jnp.arange(slot_total, dtype=jnp.int32)[:, None]).astype(
        jnp.bfloat16
    )

    feature_start = lax.axis_index("tensor") * feature_total
    hidden_shard = lax.dynamic_slice_in_dim(hidden, feature_start, feature_total, 2)
    gain_shard = lax.dynamic_slice_in_dim(input_norm_gain, feature_start, feature_total, 0)
    own_features = (
        hidden_shard.astype(jnp.float32) * row_scale * gain_shard.astype(jnp.float32)
    ).astype(jnp.bfloat16)
    packed = jnp.dot(
        pick,
        own_features.reshape(row_count, token_count * feature_total),
        preferred_element_type=jnp.float32,
    ).astype(jnp.bfloat16)
    packed = packed.reshape(owner_count, cap * token_count, feature_total)
    slot_adapter = jnp.dot(
        pick, local_adapter.astype(jnp.bfloat16), preferred_element_type=jnp.float32
    ).astype(jnp.bfloat16)
    id_row = jnp.zeros((owner_count, 1, feature_total), jnp.bfloat16)
    id_row = lax.dynamic_update_slice(
        id_row, slot_adapter.reshape(owner_count, 1, cap), (0, 0, 0)
    )
    send = jnp.concatenate([packed, id_row], axis=1)
    recv = lax.all_to_all(send, "adapter", 0, 0, tiled=True)

    got_rows = recv[:, : cap * token_count].reshape(slot_total, token_count, feature_total)
    got_adapter = recv[:, cap * token_count, :cap].reshape(slot_total).astype(jnp.int32)
    selector = (
        got_adapter[:, None] == jnp.arange(adapter_number, dtype=jnp.int32)[None, :]
    ).astype(jnp.float32)

    down_all = jnp.einsum(
        "euz,nzs->euns", got_rows, adapter_down_weight, preferred_element_type=jnp.float32
    )
    partial_rank = jnp.sum(down_all * selector[:, None, :, None], axis=2)
    rank_hidden = butterfly_sum(partial_rank, "tensor").astype(jnp.bfloat16)

    rank_selector = selector.astype(jnp.bfloat16)
    masked = rank_hidden[:, :, None, :] * rank_selector[:, None, :, None]
    key_part = jnp.einsum(
        "gled,edb->glb",
        masked[..., :rank_width],
        adapter_up_weight[:, 0],
        preferred_element_type=jnp.float32,
    )
    value_part = jnp.einsum(
        "gled,edb->glb",
        masked[..., rank_width:],
        adapter_up_weight[:, 1],
        preferred_element_type=jnp.float32,
    )
    delta_slots = jnp.stack([key_part, value_part], axis=2)
    delta_send = delta_slots.reshape(owner_count, cap * token_count * 2, column_count)
    delta_recv = lax.all_to_all(delta_send, "adapter", 0, 0, tiled=True)
    delta_rows = delta_recv.reshape(slot_total, token_count * 2 * column_count)
    adapter_update = jnp.dot(
        pick.astype(jnp.float32).T,
        delta_rows,
        precision=lax.Precision.HIGHEST,
        preferred_element_type=jnp.float32,
    ).reshape(row_count, token_count, 2, column_count)

    projected_output = base_proj + adapter_update
    positions = (cached_length[:, None] + jnp.arange(token_count, dtype=jnp.int32)[None, :]).astype(
        jnp.float32
    )
    kv_local = column_count // HEAD_DIM
    key_vecs = rotate_keys(
        projected_output[:, :, 0].reshape(row_count, token_count, kv_local, HEAD_DIM),
        positions[:, :, None],
    )
    new_keys = key_vecs.reshape(row_count, token_count, column_count).astype(jnp.bfloat16)
    new_values = projected_output[:, :, 1].astype(jnp.bfloat16)
    attended = attend(
        queries, cached_key_rows, cached_value_rows, cached_length, new_keys, new_values, HEAD_DIM
    )
    return (new_keys, new_values, attended)


def solution(mesh):
    in_specs = (
        P("adapter", None, None),
        P(),
        P(None, None, "tensor"),
        P("adapter", "tensor", None),
        P("adapter", None, None, "tensor"),
        P("adapter"),
        P("adapter", None, "tensor"),
        P("adapter", None, "tensor"),
        P("adapter", None, "tensor"),
        P("adapter"),
    )
    out_specs = (
        P("adapter", None, "tensor"),
        P("adapter", None, "tensor"),
        P("adapter", None, "tensor"),
    )
    return jax.shard_map(body, mesh=mesh, in_specs=in_specs, out_specs=out_specs, check_vma=False)
```

```python
import jax
import jax.numpy as jnp
from jax import lax
from jax.sharding import PartitionSpec as P

HEAD_DIM = 128
SLOT_CAPACITY = 6


epsilon = 1e-05
rope_base = 500000.0


def rotate_keys(key_vecs, positions):
    head_size = key_vecs.shape[-1]
    half_size = head_size // 2
    inverse = rope_base ** (-(jnp.arange(half_size, dtype=jnp.float32) * 2.0 / head_size))
    angles = positions[..., None] * inverse
    cosine = jnp.cos(angles)
    sine_part = jnp.sin(angles)
    first_half = key_vecs[..., :half_size]
    second = key_vecs[..., half_size:]
    return jnp.concatenate(
        [first_half * cosine - second * sine_part, second * cosine + first_half * sine_part],
        axis=-1,
    )


def normalize(hidden, input_norm_gain):
    values = hidden.astype(jnp.float32)
    meansq = jnp.mean(values * values, axis=-1, keepdims=True)
    return (values * lax.rsqrt(meansq + epsilon) * input_norm_gain.astype(jnp.float32)).astype(
        jnp.bfloat16
    )


def attend(
    queries, cached_key_rows, cached_value_rows, cached_length, new_keys, new_values, head_size
):
    row_total, token_total, query_width = queries.shape
    context = cached_key_rows.shape[1]
    kv_local = cached_key_rows.shape[2] // head_size
    group_size = query_width // (kv_local * head_size)
    score_scale = float(head_size) ** (-0.5)
    query_vecs = queries.reshape(row_total, token_total, kv_local, group_size, head_size)
    cache_vecs = cached_key_rows.reshape(row_total, context, kv_local, head_size)
    fresh_vecs = new_keys.reshape(row_total, token_total, kv_local, head_size)
    cache_scores = (
        jnp.einsum("rthgd,rjhd->rthgj", query_vecs, cache_vecs, preferred_element_type=jnp.float32)
        * score_scale
    )
    slot_live = jnp.arange(context, dtype=jnp.int32)[None, :] < cached_length[:, None]
    cache_scores = jnp.where(slot_live[:, None, None, None, :], cache_scores, -1e30)
    fresh_scores = (
        jnp.einsum("rthgd,rshd->rthgs", query_vecs, fresh_vecs, preferred_element_type=jnp.float32)
        * score_scale
    )
    causal = (
        jnp.arange(token_total, dtype=jnp.int32)[:, None]
        >= jnp.arange(token_total, dtype=jnp.int32)[None, :]
    )
    fresh_scores = jnp.where(causal[None, :, None, None, :], fresh_scores, -1e30)
    top_score = jnp.maximum(jnp.max(cache_scores, axis=-1), jnp.max(fresh_scores, axis=-1))[
        ..., None
    ]
    cache_weights = jnp.exp(cache_scores - top_score)
    fresh_weights = jnp.exp(fresh_scores - top_score)
    total_weight = jnp.sum(cache_weights, axis=-1, keepdims=True) + jnp.sum(
        fresh_weights, axis=-1, keepdims=True
    )
    cache_probs = (cache_weights / total_weight).astype(jnp.bfloat16)
    fresh_probs = (fresh_weights / total_weight).astype(jnp.bfloat16)
    cache_vals = cached_value_rows.reshape(row_total, context, kv_local, head_size)
    fresh_vals = new_values.reshape(row_total, token_total, kv_local, head_size)
    mixed_out = jnp.einsum(
        "rthgj,rjhd->rthgd", cache_probs, cache_vals, preferred_element_type=jnp.float32
    )
    mixed_out = mixed_out + jnp.einsum(
        "rthgs,rshd->rthgd", fresh_probs, fresh_vals, preferred_element_type=jnp.float32
    )
    return mixed_out.reshape(row_total, token_total, query_width).astype(jnp.bfloat16)


def butterfly_sum(value, axis_name):
    member_count = lax.axis_size(axis_name)
    value = value + lax.ppermute(value, axis_name, [(i, i ^ 1) for i in range(member_count)])
    shifted = [
        lax.ppermute(value, axis_name, [(i, (i + 2 * k) % member_count) for i in range(member_count)])
        for k in (1, 2, 3)
    ]
    return (value + shifted[1]) + (shifted[0] + shifted[2])


def body(
    hidden,
    input_norm_gain,
    key_value_weight,
    adapter_down_weight,
    adapter_up_weight,
    request_adapter,
    queries,
    cached_key_rows,
    cached_value_rows,
    cached_length,
):
    row_count, token_count, model_width = hidden.shape
    feature_total = adapter_down_weight.shape[1]
    adapter_number = adapter_down_weight.shape[0]
    rank_total = adapter_down_weight.shape[2]
    rank_width = adapter_up_weight.shape[2]
    column_count = key_value_weight.shape[2]
    owner_count = lax.axis_size("adapter")
    cap = SLOT_CAPACITY
    slot_total = owner_count * cap

    values = hidden.astype(jnp.float32)
    meansq = jnp.mean(values * values, axis=-1, keepdims=True)
    row_scale = lax.rsqrt(meansq + epsilon)
    normed_input = (values * row_scale * input_norm_gain.astype(jnp.float32)).astype(jnp.bfloat16)
    base_proj = jnp.dot(
        normed_input.reshape(row_count * token_count, model_width),
        key_value_weight.reshape(model_width, 2 * column_count),
        preferred_element_type=jnp.float32,
    )
    base_proj = lax.optimization_barrier(base_proj.reshape(row_count, token_count, 2, column_count))

    owner_of = request_adapter // adapter_number
    local_adapter = request_adapter - owner_of * adapter_number
    row_ids = jnp.arange(row_count, dtype=jnp.int32)
    same_owner = owner_of[:, None] == owner_of[None, :]
    earlier = row_ids[None, :] < row_ids[:, None]
    rank_in_owner = jnp.sum((same_owner & earlier).astype(jnp.int32), axis=1)
    slot_of = owner_of * cap + rank_in_owner
    pick = (slot_of[None, :] == jnp.arange(slot_total, dtype=jnp.int32)[:, None]).astype(
        jnp.bfloat16
    )

    feature_start = lax.axis_index("tensor") * feature_total
    hidden_shard = lax.dynamic_slice_in_dim(hidden, feature_start, feature_total, 2)
    gain_shard = lax.dynamic_slice_in_dim(input_norm_gain, feature_start, feature_total, 0)
    own_features = (
        hidden_shard.astype(jnp.float32) * row_scale * gain_shard.astype(jnp.float32)
    ).astype(jnp.bfloat16)
    packed = jnp.dot(
        pick,
        own_features.reshape(row_count, token_count * feature_total),
        preferred_element_type=jnp.float32,
    ).astype(jnp.bfloat16)
    packed = packed.reshape(owner_count, cap * token_count, feature_total)
    slot_adapter = jnp.dot(
        pick, local_adapter.astype(jnp.bfloat16), preferred_element_type=jnp.float32
    ).astype(jnp.bfloat16)
    id_row = jnp.zeros((owner_count, 1, feature_total), jnp.bfloat16)
    id_row = lax.dynamic_update_slice(
        id_row, slot_adapter.reshape(owner_count, 1, cap), (0, 0, 0)
    )
    send = jnp.concatenate([packed, id_row], axis=1)
    recv = lax.all_to_all(send, "adapter", 0, 0, tiled=True)

    got_rows = recv[:, : cap * token_count].reshape(slot_total, token_count, feature_total)
    got_adapter = recv[:, cap * token_count, :cap].reshape(slot_total).astype(jnp.int32)
    selector = (
        got_adapter[:, None] == jnp.arange(adapter_number, dtype=jnp.int32)[None, :]
    ).astype(jnp.float32)

    down_all = jnp.einsum(
        "euz,nzs->euns", got_rows, adapter_down_weight, preferred_element_type=jnp.float32
    )
    partial_rank = jnp.sum(down_all * selector[:, None, :, None], axis=2)
    partial_rank, base_proj = lax.optimization_barrier((partial_rank, base_proj))
    rank_hidden = butterfly_sum(partial_rank, "tensor").astype(jnp.bfloat16)

    rank_selector = selector.astype(jnp.bfloat16)
    masked = rank_hidden[:, :, None, :] * rank_selector[:, None, :, None]
    key_part = jnp.einsum(
        "gled,edb->glb",
        masked[..., :rank_width],
        adapter_up_weight[:, 0],
        preferred_element_type=jnp.float32,
    )
    value_part = jnp.einsum(
        "gled,edb->glb",
        masked[..., rank_width:],
        adapter_up_weight[:, 1],
        preferred_element_type=jnp.float32,
    )
    delta_slots = jnp.stack([key_part, value_part], axis=2)
    delta_send = delta_slots.reshape(owner_count, cap * token_count * 2, column_count)
    delta_recv = lax.all_to_all(delta_send, "adapter", 0, 0, tiled=True)
    delta_rows = delta_recv.reshape(slot_total, token_count * 2 * column_count)
    adapter_update = jnp.dot(
        pick.astype(jnp.float32).T,
        delta_rows,
        precision=lax.Precision.HIGHEST,
        preferred_element_type=jnp.float32,
    ).reshape(row_count, token_count, 2, column_count)

    projected_output = base_proj + adapter_update
    positions = (cached_length[:, None] + jnp.arange(token_count, dtype=jnp.int32)[None, :]).astype(
        jnp.float32
    )
    kv_local = column_count // HEAD_DIM
    key_vecs = rotate_keys(
        projected_output[:, :, 0].reshape(row_count, token_count, kv_local, HEAD_DIM),
        positions[:, :, None],
    )
    new_keys = key_vecs.reshape(row_count, token_count, column_count).astype(jnp.bfloat16)
    new_values = projected_output[:, :, 1].astype(jnp.bfloat16)
    attended = attend(
        queries, cached_key_rows, cached_value_rows, cached_length, new_keys, new_values, HEAD_DIM
    )
    return (new_keys, new_values, attended)


def solution(mesh):
    in_specs = (
        P("adapter", None, None),
        P(),
        P(None, None, "tensor"),
        P("adapter", "tensor", None),
        P("adapter", None, None, "tensor"),
        P("adapter"),
        P("adapter", None, "tensor"),
        P("adapter", None, "tensor"),
        P("adapter", None, "tensor"),
        P("adapter"),
    )
    out_specs = (
        P("adapter", None, "tensor"),
        P("adapter", None, "tensor"),
        P("adapter", None, "tensor"),
    )
    return jax.shard_map(body, mesh=mesh, in_specs=in_specs, out_specs=out_specs, check_vma=False)
```

```python
import jax
import jax.numpy as jnp
from jax import lax
from jax.sharding import PartitionSpec as P

HEAD_DIM = 128
SLOT_CAPACITY = 6


epsilon = 1e-05
rope_base = 500000.0


def rotate_keys(key_vecs, positions):
    head_size = key_vecs.shape[-1]
    half_size = head_size // 2
    inverse = rope_base ** (-(jnp.arange(half_size, dtype=jnp.float32) * 2.0 / head_size))
    angles = positions[..., None] * inverse
    cosine = jnp.cos(angles)
    sine_part = jnp.sin(angles)
    first_half = key_vecs[..., :half_size]
    second = key_vecs[..., half_size:]
    return jnp.concatenate(
        [first_half * cosine - second * sine_part, second * cosine + first_half * sine_part],
        axis=-1,
    )


def normalize(hidden, input_norm_gain):
    values = hidden.astype(jnp.float32)
    meansq = jnp.mean(values * values, axis=-1, keepdims=True)
    return (values * lax.rsqrt(meansq + epsilon) * input_norm_gain.astype(jnp.float32)).astype(
        jnp.bfloat16
    )


def attend(
    queries, cached_key_rows, cached_value_rows, cached_length, new_keys, new_values, head_size
):
    row_total, token_total, query_width = queries.shape
    context = cached_key_rows.shape[1]
    kv_local = cached_key_rows.shape[2] // head_size
    group_size = query_width // (kv_local * head_size)
    score_scale = float(head_size) ** (-0.5)
    query_vecs = queries.reshape(row_total, token_total, kv_local, group_size, head_size)
    cache_vecs = cached_key_rows.reshape(row_total, context, kv_local, head_size)
    fresh_vecs = new_keys.reshape(row_total, token_total, kv_local, head_size)
    cache_scores = (
        jnp.einsum("rthgd,rjhd->rthgj", query_vecs, cache_vecs, preferred_element_type=jnp.float32)
        * score_scale
    )
    slot_live = jnp.arange(context, dtype=jnp.int32)[None, :] < cached_length[:, None]
    cache_scores = jnp.where(slot_live[:, None, None, None, :], cache_scores, -1e30)
    every_fresh = jnp.einsum(
        "rthgd,ushd->rthgus", query_vecs, fresh_vecs, preferred_element_type=jnp.float32
    )
    own_request = (
        jnp.arange(row_total, dtype=jnp.int32)[:, None]
        == jnp.arange(row_total, dtype=jnp.int32)[None, :]
    )
    fresh_scores = (
        jnp.sum(
            jnp.where(own_request[:, None, None, None, :, None], every_fresh, 0.0), axis=4
        )
        * score_scale
    )
    causal = (
        jnp.arange(token_total, dtype=jnp.int32)[:, None]
        >= jnp.arange(token_total, dtype=jnp.int32)[None, :]
    )
    fresh_scores = jnp.where(causal[None, :, None, None, :], fresh_scores, -1e30)
    top_score = jnp.maximum(jnp.max(cache_scores, axis=-1), jnp.max(fresh_scores, axis=-1))[
        ..., None
    ]
    cache_weights = jnp.exp(cache_scores - top_score)
    fresh_weights = jnp.exp(fresh_scores - top_score)
    total_weight = jnp.sum(cache_weights, axis=-1, keepdims=True) + jnp.sum(
        fresh_weights, axis=-1, keepdims=True
    )
    cache_probs = (cache_weights / total_weight).astype(jnp.bfloat16)
    fresh_probs = (fresh_weights / total_weight).astype(jnp.bfloat16)
    cache_vals = cached_value_rows.reshape(row_total, context, kv_local, head_size)
    fresh_vals = new_values.reshape(row_total, token_total, kv_local, head_size)
    mixed_out = jnp.einsum(
        "rthgj,rjhd->rthgd", cache_probs, cache_vals, preferred_element_type=jnp.float32
    )
    mixed_out = mixed_out + jnp.einsum(
        "rthgs,rshd->rthgd", fresh_probs, fresh_vals, preferred_element_type=jnp.float32
    )
    return mixed_out.reshape(row_total, token_total, query_width).astype(jnp.bfloat16)


def butterfly_sum(value, axis_name):
    member_count = lax.axis_size(axis_name)
    value = value + lax.ppermute(value, axis_name, [(i, i ^ 1) for i in range(member_count)])
    shifted = [
        lax.ppermute(value, axis_name, [(i, (i + 2 * k) % member_count) for i in range(member_count)])
        for k in (1, 2, 3)
    ]
    return (value + shifted[1]) + (shifted[0] + shifted[2])


def body(
    hidden,
    input_norm_gain,
    key_value_weight,
    adapter_down_weight,
    adapter_up_weight,
    request_adapter,
    queries,
    cached_key_rows,
    cached_value_rows,
    cached_length,
):
    row_count, token_count, model_width = hidden.shape
    feature_total = adapter_down_weight.shape[1]
    adapter_number = adapter_down_weight.shape[0]
    rank_total = adapter_down_weight.shape[2]
    rank_width = adapter_up_weight.shape[2]
    column_count = key_value_weight.shape[2]
    owner_count = lax.axis_size("adapter")
    cap = SLOT_CAPACITY
    slot_total = owner_count * cap

    values = hidden.astype(jnp.float32)
    meansq = jnp.mean(values * values, axis=-1, keepdims=True)
    row_scale = lax.rsqrt(meansq + epsilon)
    normed_input = (values * row_scale * input_norm_gain.astype(jnp.float32)).astype(jnp.bfloat16)
    base_proj = jnp.dot(
        normed_input.reshape(row_count * token_count, model_width),
        key_value_weight.reshape(model_width, 2 * column_count),
        preferred_element_type=jnp.float32,
    )
    base_proj = lax.optimization_barrier(base_proj.reshape(row_count, token_count, 2, column_count))

    owner_of = request_adapter // adapter_number
    local_adapter = request_adapter - owner_of * adapter_number
    row_ids = jnp.arange(row_count, dtype=jnp.int32)
    same_owner = owner_of[:, None] == owner_of[None, :]
    earlier = row_ids[None, :] < row_ids[:, None]
    rank_in_owner = jnp.sum((same_owner & earlier).astype(jnp.int32), axis=1)
    slot_of = owner_of * cap + rank_in_owner
    pick = (slot_of[None, :] == jnp.arange(slot_total, dtype=jnp.int32)[:, None]).astype(
        jnp.bfloat16
    )

    feature_start = lax.axis_index("tensor") * feature_total
    hidden_shard = lax.dynamic_slice_in_dim(hidden, feature_start, feature_total, 2)
    gain_shard = lax.dynamic_slice_in_dim(input_norm_gain, feature_start, feature_total, 0)
    own_features = (
        hidden_shard.astype(jnp.float32) * row_scale * gain_shard.astype(jnp.float32)
    ).astype(jnp.bfloat16)
    packed = jnp.dot(
        pick,
        own_features.reshape(row_count, token_count * feature_total),
        preferred_element_type=jnp.float32,
    ).astype(jnp.bfloat16)
    packed = packed.reshape(owner_count, cap * token_count, feature_total)
    slot_adapter = jnp.dot(
        pick, local_adapter.astype(jnp.bfloat16), preferred_element_type=jnp.float32
    ).astype(jnp.bfloat16)
    id_row = jnp.zeros((owner_count, 1, feature_total), jnp.bfloat16)
    id_row = lax.dynamic_update_slice(
        id_row, slot_adapter.reshape(owner_count, 1, cap), (0, 0, 0)
    )
    send = jnp.concatenate([packed, id_row], axis=1)
    recv = lax.all_to_all(send, "adapter", 0, 0, tiled=True)

    got_rows = recv[:, : cap * token_count].reshape(slot_total, token_count, feature_total)
    got_adapter = recv[:, cap * token_count, :cap].reshape(slot_total).astype(jnp.int32)
    selector = (
        got_adapter[:, None] == jnp.arange(adapter_number, dtype=jnp.int32)[None, :]
    ).astype(jnp.float32)

    down_all = jnp.einsum(
        "euz,nzs->euns", got_rows, adapter_down_weight, preferred_element_type=jnp.float32
    )
    partial_rank = jnp.sum(down_all * selector[:, None, :, None], axis=2)
    rank_hidden = butterfly_sum(partial_rank, "tensor").astype(jnp.bfloat16)

    rank_selector = selector.astype(jnp.bfloat16)
    masked = rank_hidden[:, :, None, :] * rank_selector[:, None, :, None]
    key_part = jnp.einsum(
        "gled,edb->glb",
        masked[..., :rank_width],
        adapter_up_weight[:, 0],
        preferred_element_type=jnp.float32,
    )
    value_part = jnp.einsum(
        "gled,edb->glb",
        masked[..., rank_width:],
        adapter_up_weight[:, 1],
        preferred_element_type=jnp.float32,
    )
    delta_slots = jnp.stack([key_part, value_part], axis=2)
    delta_send = delta_slots.reshape(owner_count, cap * token_count * 2, column_count)
    delta_recv = lax.all_to_all(delta_send, "adapter", 0, 0, tiled=True)
    delta_rows = delta_recv.reshape(slot_total, token_count * 2 * column_count)
    adapter_update = jnp.take(delta_rows, slot_of, axis=0).reshape(
        row_count, token_count, 2, column_count
    )

    projected_output = base_proj + adapter_update
    positions = (cached_length[:, None] + jnp.arange(token_count, dtype=jnp.int32)[None, :]).astype(
        jnp.float32
    )
    kv_local = column_count // HEAD_DIM
    key_vecs = rotate_keys(
        projected_output[:, :, 0].reshape(row_count, token_count, kv_local, HEAD_DIM),
        positions[:, :, None],
    )
    new_keys = key_vecs.reshape(row_count, token_count, column_count).astype(jnp.bfloat16)
    new_values = projected_output[:, :, 1].astype(jnp.bfloat16)
    attended = attend(
        queries, cached_key_rows, cached_value_rows, cached_length, new_keys, new_values, HEAD_DIM
    )
    return (new_keys, new_values, attended)


def solution(mesh):
    in_specs = (
        P("adapter", None, None),
        P(),
        P(None, None, "tensor"),
        P("adapter", "tensor", None),
        P("adapter", None, None, "tensor"),
        P("adapter"),
        P("adapter", None, "tensor"),
        P("adapter", None, "tensor"),
        P("adapter", None, "tensor"),
        P("adapter"),
    )
    out_specs = (
        P("adapter", None, "tensor"),
        P("adapter", None, "tensor"),
        P("adapter", None, "tensor"),
    )
    return jax.shard_map(body, mesh=mesh, in_specs=in_specs, out_specs=out_specs, check_vma=False)
```

```python
import jax
import jax.numpy as jnp
from jax import lax
from jax.sharding import PartitionSpec as P

HEAD_DIM = 128
SLOT_CAPACITY = 6


epsilon = 1e-05
rope_base = 500000.0


def rotate_keys(key_vecs, positions):
    head_size = key_vecs.shape[-1]
    half_size = head_size // 2
    inverse = rope_base ** (-(jnp.arange(half_size, dtype=jnp.float32) * 2.0 / head_size))
    angles = positions[..., None] * inverse
    cosine = jnp.cos(angles)
    sine_part = jnp.sin(angles)
    first_half = key_vecs[..., :half_size]
    second = key_vecs[..., half_size:]
    return jnp.concatenate(
        [first_half * cosine - second * sine_part, second * cosine + first_half * sine_part],
        axis=-1,
    )


def normalize(hidden, input_norm_gain):
    values = hidden.astype(jnp.float32)
    meansq = jnp.mean(values * values, axis=-1, keepdims=True)
    return (values * lax.rsqrt(meansq + epsilon) * input_norm_gain.astype(jnp.float32)).astype(
        jnp.bfloat16
    )


def attend(
    queries, cached_key_rows, cached_value_rows, cached_length, new_keys, new_values, head_size
):
    row_total, token_total, query_width = queries.shape
    context = cached_key_rows.shape[1]
    kv_local = cached_key_rows.shape[2] // head_size
    group_size = query_width // (kv_local * head_size)
    score_scale = float(head_size) ** (-0.5)
    query_vecs = queries.reshape(row_total, token_total, kv_local, group_size, head_size)
    cache_vecs = cached_key_rows.reshape(row_total, context, kv_local, head_size)
    fresh_vecs = new_keys.reshape(row_total, token_total, kv_local, head_size)
    cache_scores = (
        jnp.einsum("rthgd,rjhd->rthgj", query_vecs, cache_vecs, preferred_element_type=jnp.float32)
        * score_scale
    )
    slot_live = jnp.arange(context, dtype=jnp.int32)[None, :] < cached_length[:, None]
    cache_scores = jnp.where(slot_live[:, None, None, None, :], cache_scores, -1e30)
    fresh_scores = (
        jnp.einsum("rthgd,rshd->rthgs", query_vecs, fresh_vecs, preferred_element_type=jnp.float32)
        * score_scale
    )
    causal = (
        jnp.arange(token_total, dtype=jnp.int32)[:, None]
        >= jnp.arange(token_total, dtype=jnp.int32)[None, :]
    )
    fresh_scores = jnp.where(causal[None, :, None, None, :], fresh_scores, -1e30)
    top_score = jnp.maximum(jnp.max(cache_scores, axis=-1), jnp.max(fresh_scores, axis=-1))[
        ..., None
    ]
    cache_weights = jnp.exp(cache_scores - top_score)
    fresh_weights = jnp.exp(fresh_scores - top_score)
    total_weight = jnp.sum(cache_weights, axis=-1, keepdims=True) + jnp.sum(
        fresh_weights, axis=-1, keepdims=True
    )
    cache_probs = (cache_weights / total_weight).astype(jnp.bfloat16)
    fresh_probs = (fresh_weights / total_weight).astype(jnp.bfloat16)
    cache_vals = cached_value_rows.reshape(row_total, context, kv_local, head_size)
    fresh_vals = new_values.reshape(row_total, token_total, kv_local, head_size)
    mixed_out = jnp.einsum(
        "rthgj,rjhd->rthgd", cache_probs, cache_vals, preferred_element_type=jnp.float32
    )
    mixed_out = mixed_out + jnp.einsum(
        "rthgs,rshd->rthgd", fresh_probs, fresh_vals, preferred_element_type=jnp.float32
    )
    return mixed_out.reshape(row_total, token_total, query_width).astype(jnp.bfloat16)


def butterfly_sum(value, axis_name):
    member_count = lax.axis_size(axis_name)
    value = value + lax.ppermute(value, axis_name, [(i, i ^ 1) for i in range(member_count)])
    shifted = [
        lax.ppermute(value, axis_name, [(i, (i + 2 * k) % member_count) for i in range(member_count)])
        for k in (1, 2, 3)
    ]
    return (value + shifted[1]) + (shifted[0] + shifted[2])


def body(
    hidden,
    input_norm_gain,
    key_value_weight,
    adapter_down_weight,
    adapter_up_weight,
    request_adapter,
    queries,
    cached_key_rows,
    cached_value_rows,
    cached_length,
):
    row_count, token_count, model_width = hidden.shape
    feature_total = adapter_down_weight.shape[1]
    adapter_number = adapter_down_weight.shape[0]
    rank_total = adapter_down_weight.shape[2]
    rank_width = adapter_up_weight.shape[2]
    column_count = key_value_weight.shape[2]
    owner_count = lax.axis_size("adapter")
    cap = SLOT_CAPACITY
    slot_total = owner_count * cap

    values = hidden.astype(jnp.float32)
    meansq = jnp.mean(values * values, axis=-1, keepdims=True)
    row_scale = lax.rsqrt(meansq + epsilon)
    normed_input = (values * row_scale * input_norm_gain.astype(jnp.float32)).astype(jnp.bfloat16)
    base_proj = jnp.dot(
        normed_input.reshape(row_count * token_count, model_width),
        key_value_weight.reshape(model_width, 2 * column_count),
        preferred_element_type=jnp.float32,
    )
    base_proj = lax.optimization_barrier(base_proj.reshape(row_count, token_count, 2, column_count))

    owner_of = request_adapter // adapter_number
    local_adapter = request_adapter - owner_of * adapter_number
    row_ids = jnp.arange(row_count, dtype=jnp.int32)
    same_owner = owner_of[:, None] == owner_of[None, :]
    earlier = row_ids[None, :] < row_ids[:, None]
    rank_in_owner = jnp.sum((same_owner & earlier).astype(jnp.int32), axis=1)
    slot_of = owner_of * cap + rank_in_owner
    pick = (slot_of[None, :] == jnp.arange(slot_total, dtype=jnp.int32)[:, None]).astype(
        jnp.bfloat16
    )

    feature_start = lax.axis_index("tensor") * feature_total
    hidden_shard = lax.dynamic_slice_in_dim(hidden, feature_start, feature_total, 2)
    gain_shard = lax.dynamic_slice_in_dim(input_norm_gain, feature_start, feature_total, 0)
    own_features = (
        hidden_shard.astype(jnp.float32) * row_scale * gain_shard.astype(jnp.float32)
    ).astype(jnp.bfloat16)
    packed = jnp.dot(
        pick,
        own_features.reshape(row_count, token_count * feature_total),
        preferred_element_type=jnp.float32,
    ).astype(jnp.bfloat16)
    packed = packed.reshape(owner_count, cap * token_count, feature_total)
    slot_adapter = jnp.dot(
        pick, local_adapter.astype(jnp.bfloat16), preferred_element_type=jnp.float32
    ).astype(jnp.bfloat16)
    id_row = jnp.zeros((owner_count, 1, feature_total), jnp.bfloat16)
    id_row = lax.dynamic_update_slice(
        id_row, slot_adapter.reshape(owner_count, 1, cap), (0, 0, 0)
    )
    send = jnp.concatenate([packed, id_row], axis=1)
    recv = lax.all_to_all(send, "adapter", 0, 0, tiled=True)

    got_rows = recv[:, : cap * token_count]
    got_adapter = recv[:, cap * token_count, :cap].reshape(slot_total).astype(jnp.int32)
    selector = (
        got_adapter[:, None] == jnp.arange(adapter_number, dtype=jnp.int32)[None, :]
    ).astype(jnp.float32)
    row_selector = jnp.repeat(
        selector.reshape(owner_count, cap, adapter_number), token_count, axis=1
    )

    down_all = jnp.einsum(
        "qjz,nzs->qjns", got_rows, adapter_down_weight, preferred_element_type=jnp.float32
    )
    partial_rank = jnp.sum(down_all * row_selector[..., None], axis=2)
    rank_hidden = butterfly_sum(partial_rank, "tensor").astype(jnp.bfloat16)

    masked = rank_hidden[:, :, None, :] * row_selector.astype(jnp.bfloat16)[..., None]
    key_part = jnp.einsum(
        "qjed,edb->qjb",
        masked[..., :rank_width],
        adapter_up_weight[:, 0],
        preferred_element_type=jnp.float32,
    )
    value_part = jnp.einsum(
        "qjed,edb->qjb",
        masked[..., rank_width:],
        adapter_up_weight[:, 1],
        preferred_element_type=jnp.float32,
    )
    delta_slots = jnp.stack([key_part, value_part], axis=2)
    delta_send = delta_slots.reshape(owner_count, cap * token_count * 2, column_count)
    delta_recv = lax.all_to_all(delta_send, "adapter", 0, 0, tiled=True)
    delta_rows = delta_recv.reshape(slot_total, token_count * 2 * column_count)
    adapter_update = jnp.take(delta_rows, slot_of, axis=0).reshape(
        row_count, token_count, 2, column_count
    )

    projected_output = base_proj + adapter_update
    positions = (cached_length[:, None] + jnp.arange(token_count, dtype=jnp.int32)[None, :]).astype(
        jnp.float32
    )
    kv_local = column_count // HEAD_DIM
    key_vecs = rotate_keys(
        projected_output[:, :, 0].reshape(row_count, token_count, kv_local, HEAD_DIM),
        positions[:, :, None],
    )
    new_keys = key_vecs.reshape(row_count, token_count, column_count).astype(jnp.bfloat16)
    new_values = projected_output[:, :, 1].astype(jnp.bfloat16)
    attended = attend(
        queries, cached_key_rows, cached_value_rows, cached_length, new_keys, new_values, HEAD_DIM
    )
    return (new_keys, new_values, attended)


def solution(mesh):
    in_specs = (
        P("adapter", None, None),
        P(),
        P(None, None, "tensor"),
        P("adapter", "tensor", None),
        P("adapter", None, None, "tensor"),
        P("adapter"),
        P("adapter", None, "tensor"),
        P("adapter", None, "tensor"),
        P("adapter", None, "tensor"),
        P("adapter"),
    )
    out_specs = (
        P("adapter", None, "tensor"),
        P("adapter", None, "tensor"),
        P("adapter", None, "tensor"),
    )
    return jax.shard_map(body, mesh=mesh, in_specs=in_specs, out_specs=out_specs, check_vma=False)
```
